256 devices in a mesh: seq: 128 (over x, y, z), head: 2 (over core).
Axes of the slice: x: 4, y: 4, z: 8, core: 2. Of those that a mesh axis runs over, the one named last changes fastest.
Arguments:
- queries: bfloat16 [32768, 4096], P('seq', 'head'), may hold values from -12 to 12
- key_states: bfloat16 [32768, 1024], P('seq', 'head'), may hold values from -12 to 12
- value_states: bfloat16 [32768, 1024], P('seq', 'head'), may hold values from -6 to 6
- positions: int32 [3, 32768], P(None, 'seq'), may hold values from 0 to 4095
- random_blocks: int32 [512, 8, 3], P('seq', 'head'), may hold values from 0 to 511, as said below
- global_blocks: int32 [2], replicated, may hold values from 0 to 511
- out_grad: bfloat16 [32768, 4096], P('seq', 'head'), may hold values from -6 to 6
Outputs:
- attended: bfloat16 [32768, 4096], P('seq', 'head')
- query_grad: bfloat16 [32768, 4096], P('seq', 'head')
- key_grad: bfloat16 [32768, 1024], P('seq', 'head')
- value_grad: bfloat16 [32768, 1024], P('seq', 'head')
The draws below stay inside these ranges and needn't reach their ends.
Inputs may be any that keep to these rules, and one draw needn't show every extreme that they name: `random_blocks`: for each index of seq and each index of head (its 4 block rows and 4 key-value heads), at most 2 of its random blocks lie in the blocks of any one index of seq, and exactly 2 in one of them.
All inputs are finite; a program needn't handle non-finite values.
Results may differ from the reference program's by a relative error of at most 0.013.
The reference program's roundings to bfloat16 on the way count: a program that leaves them out, or rounds other values in their place, can miss the bound.
Values may be sent and summed in bfloat16 or wider, within the bound.
No kernel may reach another device: no remote copies, remote signals or barrier semaphores. Data moves between devices by JAX's collectives and lax.ppermute only.
A program may use at most 128 MiB of HBM per device.

```python
import math
import jax
import jax.numpy as jnp
from jax import lax

HD = 128
GROUP = 4
KV_DEV = 4
BLK = 64
GLOB = 2
RND = 3
BLK_DEV = 4
KVH = 8
QH = 32
TOKENS = 32768
NBLK = 512
CAP = 2


def draw_queries(key, part):
    base_draw = jnp.clip(jax.random.normal(key, (TOKENS, QH, HD), jnp.float32), -6.0, 6.0)
    return base_draw.reshape(TOKENS, QH * HD).astype(jnp.bfloat16)


def draw_key_states(key, part):
    base_draw = jnp.clip(jax.random.normal(key, (TOKENS, KVH, HD), jnp.float32), -6.0, 6.0)
    return base_draw.reshape(TOKENS, KVH * HD).astype(jnp.bfloat16)


def draw_random_blocks(key, part):
    seq_count = NBLK // BLK_DEV
    head_count = KVH // KV_DEV
    slot_count = BLK_DEV * KV_DEV * RND

    def one_group(group_index):
        group_key = jax.random.fold_in(jax.random.fold_in(key, 7), group_index)
        key_order, key_spread, key_shuffle, key_local = jax.random.split(group_key, 4)
        owner_order = jax.random.permutation(key_order, seq_count).astype(jnp.int32)
        spread = jax.random.permutation(key_spread, CAP * (seq_count - 1))[:slot_count - CAP]
        owners = jnp.concatenate([jnp.full((CAP,), owner_order[0], jnp.int32), owner_order[1 + spread // CAP]])
        owners = owners[jax.random.permutation(key_shuffle, slot_count)]
        local_blocks = jax.random.randint(key_local, (slot_count,), 0, BLK_DEV, dtype=jnp.int32)
        return (owners * BLK_DEV + local_blocks).reshape(BLK_DEV, KV_DEV, RND)
    groups = jax.vmap(one_group)(jnp.arange(seq_count * head_count))
    groups = groups.reshape(seq_count, head_count, BLK_DEV, KV_DEV, RND)
    return groups.transpose(0, 2, 1, 3, 4).reshape(NBLK, KVH, RND).astype(jnp.int32)


def plant(drawn, own_key, least, high):
    place = [jax.random.randint(jax.random.fold_in(own_key, axis), (), 0, length) for axis, length in enumerate(drawn.shape)]
    main_axis = drawn.shape.index(max(drawn.shape))
    next_to = place[:main_axis] + [(place[main_axis] + 1) % drawn.shape[main_axis]] + place[main_axis + 1:]
    return drawn.at[tuple(place)].set(least).at[tuple(next_to)].set(high)


def shard_levels(rng, extent, cuts, least, high):
    gain, own = 1.0, jax.random.fold_in(rng, 6)
    for axis_at, shards_of in cuts:
        draws = jnp.exp(jax.random.uniform(jax.random.fold_in(own, axis_at), (shards_of,), jnp.float32, least / len(cuts), high / len(cuts)))
        gain = gain * jnp.repeat(draws, extent[axis_at] // shards_of).reshape([-1 if axis == axis_at else 1 for axis in range(len(extent))])
    return gain


def centred(own_key, shape, scale, most, shards=(), kind=jnp.bfloat16):
    drawn = scale * jax.random.normal(own_key, shape, jnp.float32)
    if shards:
        drawn = drawn * shard_levels(own_key, shape, shards, -0.22, 0.18)
    return jnp.clip(drawn, -most, most).astype(kind)


def setup_inputs(seed: int = 0) -> dict:
    arg_keys = jax.random.split(jax.random.key(seed), 8)
    return {
        "queries": draw_queries(jax.random.fold_in(arg_keys[7], 71), 0),
        "key_states": draw_key_states(jax.random.fold_in(arg_keys[7], 71), 0),
        "value_states": centred(arg_keys[2], (TOKENS, KVH * HD), 1.0, 6.0, ((0, 128), (1, 2))),
        "positions": plant(jax.random.randint(arg_keys[3], (3, TOKENS), 0, 4096), jax.random.fold_in(arg_keys[3], 1), 0, 4095).astype(jnp.int32),
        "random_blocks": draw_random_blocks(jax.random.fold_in(arg_keys[7], 71), 0),
        "global_blocks": jax.random.randint(arg_keys[5], (GLOB,), 0, NBLK).astype(jnp.int32),
        "out_grad": centred(arg_keys[6], (TOKENS, QH * HD), 1.0, 6.0, ((0, 128), (1, 2))),
    }


NEG_FILL = -1e+30
ROPE_BASE = 1000000.0

def tables(positions):
    half_dim = HD // 2
    freq_ids = jnp.arange(half_dim)
    inv_freq = jnp.power(jnp.float32(ROPE_BASE), -2.0 * freq_ids.astype(jnp.float32) / HD)
    pos_float = positions.astype(jnp.float32)
    chosen = jnp.where((freq_ids % 3 == 0)[None, :], pos_float[0][:, None], jnp.where((freq_ids % 3 == 1)[None, :], pos_float[1][:, None], pos_float[2][:, None]))
    angles = chosen * inv_freq[None, :]
    return (jnp.cos(angles), jnp.sin(angles))

def rotate(states, cosines, sine_vals):
    half_dim = HD // 2
    first_half = states[..., :half_dim]
    second_half = states[..., half_dim:]
    cos_b = cosines[:, None, :]
    sin_b = sine_vals[:, None, :]
    return jnp.concatenate([first_half * cos_b - second_half * sin_b, second_half * cos_b + first_half * sin_b], axis=-1)

def unrotate(states, cosines, sine_vals):
    half_dim = HD // 2
    first_half = states[..., :half_dim]
    second_half = states[..., half_dim:]
    cos_b = cosines[:, None, :]
    sin_b = sine_vals[:, None, :]
    return jnp.concatenate([first_half * cos_b + second_half * sin_b, second_half * cos_b - first_half * sin_b], axis=-1)

def attend(query_block_view, key_block_view, value_block_view, gradient_block_view, key_mask):
    score_scale = 1.0 / math.sqrt(HD)
    query_wide = query_block_view.astype(jnp.float32)
    key_wide = key_block_view.astype(jnp.float32)
    value_wide = value_block_view.astype(jnp.float32)
    gradient_wide = gradient_block_view.astype(jnp.float32)
    logit_scores = jnp.einsum('mtyp,mop->myto', query_wide, key_wide) * score_scale
    logit_scores = jnp.where(key_mask[:, None, None, :], logit_scores, NEG_FILL)
    row_max = lax.optimization_barrier(jnp.max(logit_scores, axis=-1, keepdims=True))
    exponent = jnp.exp(logit_scores - row_max)
    probability = exponent / lax.optimization_barrier(jnp.sum(exponent, axis=-1, keepdims=True))
    attention_weights = lax.optimization_barrier(probability.astype(jnp.bfloat16))
    attended = jnp.einsum('ywiu,yuz->yiwz', attention_weights.astype(jnp.float32), value_wide).astype(jnp.bfloat16)
    attended = lax.optimization_barrier(attended)
    weight_gradient = jnp.einsum('mtyp,mop->myto', gradient_wide, value_wide)
    row_delta = lax.optimization_barrier(jnp.sum(gradient_wide * attended.astype(jnp.float32), axis=-1))
    row_delta = jnp.transpose(row_delta, (0, 2, 1))[..., None]
    score_gradient = lax.optimization_barrier((probability * (weight_gradient - row_delta) * score_scale).astype(jnp.bfloat16))
    value_portion = jnp.einsum('pcht,phca->pta', attention_weights.astype(jnp.float32), gradient_wide)
    key_portion = jnp.einsum('pcht,phca->pta', score_gradient.astype(jnp.float32), query_wide)
    query_portion = jnp.einsum('ywiu,yuz->yiwz', score_gradient.astype(jnp.float32), key_wide)
    return (attended, query_portion, key_portion, value_portion)

def reference(queries, key_states, value_states, positions, random_blocks, global_blocks, out_grad):
    tok_total = queries.shape[0]
    block_count = tok_total // BLK
    key_slots = 3 + GLOB + RND
    cosines, sine_vals = tables(positions)
    q_rot = rotate(queries.reshape(tok_total, QH, HD).astype(jnp.float32), cosines, sine_vals).astype(jnp.bfloat16)
    q_rot = lax.optimization_barrier(q_rot)
    k_rot = rotate(key_states.reshape(tok_total, KVH, HD).astype(jnp.float32), cosines, sine_vals).astype(jnp.bfloat16)
    k_rot = lax.optimization_barrier(k_rot)
    query_heads = q_rot.reshape(block_count, BLK, KVH, GROUP, HD).transpose(2, 0, 1, 3, 4)
    grad_heads = out_grad.reshape(block_count, BLK, KVH, GROUP, HD).transpose(2, 0, 1, 3, 4)
    key_heads = k_rot.reshape(block_count, BLK, KVH, HD).transpose(2, 0, 1, 3)
    value_heads = value_states.reshape(block_count, BLK, KVH, HD).transpose(2, 0, 1, 3)
    block_ids = jnp.arange(block_count, dtype=jnp.int32)
    window = block_ids[:, None] + jnp.arange(-1, 2, dtype=jnp.int32)[None, :]
    window_ok = (window >= 0) & (window < block_count)
    window = jnp.clip(window, 0, block_count - 1).astype(jnp.int32)
    glob_ids = jnp.broadcast_to(global_blocks.astype(jnp.int32)[None, :], (block_count, GLOB))
    block_ok = jnp.concatenate([window_ok, jnp.ones((block_count, GLOB + RND), dtype=bool)], axis=1)
    key_mask = jnp.repeat(block_ok, BLK, axis=1)

    def one_head(inputs):
        query_h, grad_h, key_h, value_h, random_h = inputs
        chosen = jnp.concatenate([window, glob_ids, random_h.astype(jnp.int32)], axis=1)
        key_sel = key_h[chosen].reshape(block_count, key_slots * BLK, HD)
        value_sel = value_h[chosen].reshape(block_count, key_slots * BLK, HD)
        attended, query_portion, key_portion, value_portion = attend(query_h, key_sel, value_sel, grad_h, key_mask)
        flat_ids = chosen.reshape(-1)
        key_acc = jnp.zeros((block_count, BLK, HD), jnp.float32).at[flat_ids].add(key_portion.reshape(-1, BLK, HD))
        value_acc = jnp.zeros((block_count, BLK, HD), jnp.float32).at[flat_ids].add(value_portion.reshape(-1, BLK, HD))
        return (attended, query_portion, key_acc, value_acc)
    attended, query_portion, key_acc, value_acc = lax.map(one_head, (query_heads, grad_heads, key_heads, value_heads, random_blocks.transpose(1, 0, 2)))
    attended = attended.transpose(1, 2, 0, 3, 4).reshape(tok_total, QH * HD)
    query_portion = query_portion.transpose(1, 2, 0, 3, 4).reshape(tok_total, QH, HD)
    query_grad = unrotate(query_portion, cosines, sine_vals).astype(jnp.bfloat16).reshape(tok_total, QH * HD)
    key_acc = key_acc.transpose(1, 2, 0, 3).reshape(tok_total, KVH, HD)
    key_grad = unrotate(key_acc, cosines, sine_vals).astype(jnp.bfloat16).reshape(tok_total, KVH * HD)
    value_grad = value_acc.transpose(1, 2, 0, 3).reshape(tok_total, KVH * HD).astype(jnp.bfloat16)
    return (attended, query_grad, key_grad, value_grad)
```

```python
import math

import jax
import jax.numpy as jnp
from jax import lax
from jax.sharding import PartitionSpec as P

HD = 128
GROUP = 4
BLK = 64
GLOB = 2
RND = 3


NEG_FILL = -1e30
ROPE_BASE = 1000000.0


def extended(array, sides, width):
    for axis, dim in sides:
        devices, length = (lax.axis_size(axis), array.shape[dim])
        up = [(i, (i + 1) % devices) for i in range(devices - 1)]
        down = [(j, i) for i, j in up]
        last = lax.slice_in_dim(array, length - width, length, axis=dim)
        leading = lax.slice_in_dim(array, 0, width, axis=dim)
        before = lax.ppermute(last, axis, up)
        after = lax.ppermute(leading, axis, down)
        array = jnp.concatenate([before, array, after], axis=dim)
    return array


def spread(block, axis, source):
    block = jnp.where(lax.axis_index(axis) == source, block, jnp.zeros_like(block))
    return lax.psum(block, axis)


def shifted(array, axis, by):
    devices = lax.axis_size(axis)
    pairs = [(i, i + by) for i in range(devices) if 0 <= i + by < devices]
    return lax.ppermute(array, axis, pairs)


def tables(positions):
    half_dim = HD // 2
    freq_ids = jnp.arange(half_dim)
    inv_freq = jnp.power(jnp.float32(ROPE_BASE), -2.0 * freq_ids.astype(jnp.float32) / HD)
    pos_float = positions.astype(jnp.float32)
    chosen = jnp.where(
        (freq_ids % 3 == 0)[None, :],
        pos_float[0][:, None],
        jnp.where((freq_ids % 3 == 1)[None, :], pos_float[1][:, None], pos_float[2][:, None]),
    )
    angles = chosen * inv_freq[None, :]
    return (jnp.cos(angles), jnp.sin(angles))


def rotate(states, cosines, sine_vals):
    half_dim = HD // 2
    first_half = states[..., :half_dim]
    second_half = states[..., half_dim:]
    cos_b = cosines[:, None, :]
    sin_b = sine_vals[:, None, :]
    return jnp.concatenate(
        [first_half * cos_b - second_half * sin_b, second_half * cos_b + first_half * sin_b],
        axis=-1,
    )


def unrotate(states, cosines, sine_vals):
    half_dim = HD // 2
    first_half = states[..., :half_dim]
    second_half = states[..., half_dim:]
    cos_b = cosines[:, None, :]
    sin_b = sine_vals[:, None, :]
    return jnp.concatenate(
        [first_half * cos_b + second_half * sin_b, second_half * cos_b - first_half * sin_b],
        axis=-1,
    )


def attend(query_block_view, key_block_view, value_block_view, gradient_block_view, key_mask):
    score_scale = 1.0 / math.sqrt(HD)
    logit_scores = (
        jnp.einsum(
            "mtyp,mop->myto", query_block_view, key_block_view, preferred_element_type=jnp.float32
        )
        * score_scale
    )
    logit_scores = jnp.where(key_mask[:, None, None, :], logit_scores, NEG_FILL)
    row_max = jnp.max(logit_scores, axis=-1, keepdims=True)
    exponent = jnp.exp(logit_scores - row_max)
    probability = exponent / jnp.sum(exponent, axis=-1, keepdims=True)
    attention_weights = probability.astype(jnp.bfloat16)
    attended = jnp.einsum(
        "ywiu,yuz->yiwz", attention_weights, value_block_view, preferred_element_type=jnp.float32
    ).astype(jnp.bfloat16)
    weight_gradient = jnp.einsum(
        "mtyp,mop->myto", gradient_block_view, value_block_view, preferred_element_type=jnp.float32
    )
    row_delta = jnp.sum(
        gradient_block_view.astype(jnp.float32) * attended.astype(jnp.float32), axis=-1
    )
    row_delta = jnp.transpose(row_delta, (0, 2, 1))[..., None]
    score_gradient = (probability * (weight_gradient - row_delta) * score_scale).astype(
        jnp.bfloat16
    )
    value_portion = jnp.einsum(
        "pcht,phca->pta", attention_weights, gradient_block_view, preferred_element_type=jnp.float32
    )
    key_portion = jnp.einsum(
        "pcht,phca->pta", score_gradient, query_block_view, preferred_element_type=jnp.float32
    )
    query_portion = jnp.einsum(
        "ywiu,yuz->yiwz", score_gradient, key_block_view, preferred_element_type=jnp.float32
    )
    return (attended, query_portion, key_portion, value_portion)


def onehot(ids, count):
    return (ids[:, None] == jnp.arange(count, dtype=jnp.int32)[None, :]).astype(jnp.bfloat16)


def local(queries, key_states, value_states, positions, random_blocks, global_blocks, out_grad):
    tok_rows = queries.shape[0]
    block_rows = tok_rows // BLK
    kv_dev = key_states.shape[1] // HD
    seq_count = lax.axis_size("seq")
    my_index = lax.axis_index("seq")
    slot_count = block_rows * kv_dev * RND
    capacity = (slot_count + seq_count - 1) // seq_count + 1
    score_scale = 1.0 / math.sqrt(HD)
    table_rows = block_rows * kv_dev

    all_blocks = lax.all_gather(random_blocks, "seq").reshape(seq_count, slot_count)
    head_ids = jnp.broadcast_to(
        jnp.arange(kv_dev, dtype=jnp.int32)[None, :, None], (block_rows, kv_dev, RND)
    ).reshape(slot_count)
    slot_ids = jnp.arange(slot_count, dtype=jnp.int32)
    all_owners = all_blocks // block_rows
    earlier = (all_owners[:, :, None] == all_owners[:, None, :]) & (
        slot_ids[None, None, :] < slot_ids[None, :, None]
    )
    all_rank = jnp.sum(earlier, axis=2)
    all_code = all_blocks % block_rows * kv_dev + head_ids[None, :]
    mine = all_owners == my_index
    asked_part = jnp.stack(
        [jnp.sum(jnp.where(mine & (all_rank == c), all_code, 0), axis=1) for c in range(capacity)],
        axis=1,
    )
    flat_ids = random_blocks.reshape(slot_count)
    owners = flat_ids // block_rows
    my_rank = lax.dynamic_index_in_dim(all_rank, my_index, 0, keepdims=False)
    slot_pos = owners * capacity + my_rank

    cosines, sine_vals = tables(positions)
    q_rot = rotate(
        queries.reshape(tok_rows, kv_dev * GROUP, HD).astype(jnp.float32), cosines, sine_vals
    ).astype(jnp.bfloat16)
    k_rot = rotate(
        key_states.reshape(tok_rows, kv_dev, HD).astype(jnp.float32), cosines, sine_vals
    ).astype(jnp.bfloat16)
    paired = jnp.stack([k_rot.reshape(tok_rows, kv_dev * HD), value_states])
    own_blocks = paired.reshape(2, block_rows, BLK, kv_dev, HD)

    kv_table = own_blocks.transpose(1, 3, 0, 2, 4).reshape(table_rows, 2 * BLK * HD)
    asked_flat = asked_part.reshape(seq_count * capacity)
    answers = jnp.dot(
        onehot(asked_flat, table_rows), kv_table, preferred_element_type=jnp.float32
    ).astype(jnp.bfloat16)
    padded = extended(paired, (("seq", 1),), BLK)
    window_blocks = padded.reshape(2, block_rows + 2, BLK, kv_dev, HD)
    glob_owner = global_blocks // block_rows
    glob_local = global_blocks % block_rows
    glob_pieces = []
    for which_glob in range(GLOB):
        glob_piece = lax.dynamic_index_in_dim(own_blocks, glob_local[which_glob], 1, keepdims=False)
        glob_pieces.append(spread(glob_piece, "seq", glob_owner[which_glob]))
    glob_kv = jnp.stack(glob_pieces, axis=1)
    answers, padded, glob_kv = lax.optimization_barrier((answers, padded, glob_kv))
    window_blocks = padded.reshape(2, block_rows + 2, BLK, kv_dev, HD)
    fetched = lax.all_to_all(
        answers.reshape(seq_count, capacity, 2 * BLK * HD), "seq", 0, 0, tiled=True
    ).reshape(seq_count * capacity, 2 * BLK * HD)

    window_set = jnp.stack([window_blocks[:, offset : offset + block_rows] for offset in range(3)], axis=2)
    glob_set = jnp.broadcast_to(glob_kv[:, None], (2, block_rows, GLOB, BLK, kv_dev, HD))
    near_set = jnp.concatenate([window_set, glob_set], axis=2).reshape(
        2, block_rows, (3 + GLOB) * BLK, kv_dev, HD
    )
    window_ids = (
        my_index * block_rows + jnp.arange(block_rows)[:, None] + jnp.arange(-1, 2)[None, :]
    )
    window_ok = (window_ids >= 0) & (window_ids < seq_count * block_rows)
    near_ok = jnp.concatenate([window_ok, jnp.ones((block_rows, GLOB), dtype=bool)], axis=1)
    near_mask = jnp.repeat(near_ok, BLK, axis=1)

    query_nat = q_rot.reshape(block_rows, BLK, kv_dev, GROUP, HD)
    grad_nat = out_grad.reshape(block_rows, BLK, kv_dev, GROUP, HD)
    near_k = near_set[0]
    near_v = near_set[1]
    near_scores = (
        jnp.einsum("rthgd,rkhd->rhgtk", query_nat, near_k, preferred_element_type=jnp.float32)
        * score_scale
    )
    near_scores = jnp.where(near_mask[:, None, None, None, :], near_scores, NEG_FILL)
    near_wgrad = jnp.einsum("rthgd,rkhd->rhgtk", grad_nat, near_v, preferred_element_type=jnp.float32)

    random_kv = fetched[slot_pos].reshape(block_rows, kv_dev, RND, 2, BLK, HD)
    far_k = random_kv[:, :, :, 0].reshape(block_rows, kv_dev, RND * BLK, HD)
    far_v = random_kv[:, :, :, 1].reshape(block_rows, kv_dev, RND * BLK, HD)
    far_scores = (
        jnp.einsum("rthgd,rhkd->rhgtk", query_nat, far_k, preferred_element_type=jnp.float32)
        * score_scale
    )
    far_wgrad = jnp.einsum("rthgd,rhkd->rhgtk", grad_nat, far_v, preferred_element_type=jnp.float32)
    row_max = jnp.maximum(
        jnp.max(near_scores, axis=-1, keepdims=True), jnp.max(far_scores, axis=-1, keepdims=True)
    )
    near_exp = jnp.exp(near_scores - row_max)
    far_exp = jnp.exp(far_scores - row_max)
    total = jnp.sum(near_exp, axis=-1, keepdims=True) + jnp.sum(far_exp, axis=-1, keepdims=True)
    near_prob = near_exp / total
    far_prob = far_exp / total
    near_w = near_prob.astype(jnp.bfloat16)
    far_w = far_prob.astype(jnp.bfloat16)
    attended = (
        jnp.einsum("rhgtk,rkhd->rthgd", near_w, near_v, preferred_element_type=jnp.float32)
        + jnp.einsum("rhgtk,rhkd->rthgd", far_w, far_v, preferred_element_type=jnp.float32)
    ).astype(jnp.bfloat16)
    row_delta = jnp.sum(grad_nat.astype(jnp.float32) * attended.astype(jnp.float32), axis=-1)
    row_delta = row_delta.transpose(0, 2, 3, 1)[..., None]
    near_sgrad = (near_prob * (near_wgrad - row_delta) * score_scale).astype(jnp.bfloat16)
    far_sgrad = (far_prob * (far_wgrad - row_delta) * score_scale).astype(jnp.bfloat16)

    far_kgrad = jnp.einsum("rhgtk,rthgd->rhkd", far_sgrad, query_nat, preferred_element_type=jnp.float32)
    far_vgrad = jnp.einsum("rhgtk,rthgd->rhkd", far_w, grad_nat, preferred_element_type=jnp.float32)
    random_grad = jnp.stack(
        [
            far_kgrad.reshape(block_rows, kv_dev, RND, BLK, HD),
            far_vgrad.reshape(block_rows, kv_dev, RND, BLK, HD),
        ],
        axis=3,
    ).reshape(slot_count, 2 * BLK * HD).astype(jnp.bfloat16)
    outgoing = jnp.dot(
        onehot(slot_pos, seq_count * capacity).T, random_grad, preferred_element_type=jnp.float32
    ).astype(jnp.bfloat16)
    query_portion = jnp.einsum(
        "rhgtk,rkhd->rthgd", near_sgrad, near_k, preferred_element_type=jnp.float32
    ) + jnp.einsum("rhgtk,rhkd->rthgd", far_sgrad, far_k, preferred_element_type=jnp.float32)
    near_kgrad = jnp.einsum("rhgtk,rthgd->rkhd", near_sgrad, query_nat, preferred_element_type=jnp.float32)
    near_vgrad = jnp.einsum("rhgtk,rthgd->rkhd", near_w, grad_nat, preferred_element_type=jnp.float32)
    near_grad = jnp.stack([near_kgrad, near_vgrad]).reshape(2, block_rows, 3 + GLOB, BLK, kv_dev, HD)
    window_acc = jnp.pad(near_grad[:, :, 0], ((0, 0), (0, 2), (0, 0), (0, 0), (0, 0)))
    window_acc = window_acc + jnp.pad(near_grad[:, :, 1], ((0, 0), (1, 1), (0, 0), (0, 0), (0, 0)))
    window_acc = window_acc + jnp.pad(near_grad[:, :, 2], ((0, 0), (2, 0), (0, 0), (0, 0), (0, 0)))
    glob_local_grad = jnp.sum(near_grad[:, :, 3:], axis=1)
    from_right = shifted(window_acc[:, 0].astype(jnp.bfloat16), "seq", -1).astype(jnp.float32)
    from_left = shifted(window_acc[:, block_rows + 1].astype(jnp.bfloat16), "seq", 1).astype(jnp.float32)
    glob_grad = lax.psum(glob_local_grad, "seq")
    outgoing, from_right, from_left, glob_grad = lax.optimization_barrier(
        (outgoing, from_right, from_left, glob_grad)
    )
    returned = lax.all_to_all(
        outgoing.reshape(seq_count, capacity, 2 * BLK * HD), "seq", 0, 0, tiled=True
    ).reshape(seq_count * capacity, 2 * BLK * HD)

    kv_grad = window_acc[:, 1 : block_rows + 1]
    kv_grad = kv_grad.at[:, block_rows - 1].add(from_right).at[:, 0].add(from_left)
    glob_mine = jnp.where((glob_owner == my_index)[None, :, None, None, None], glob_grad, 0.0)
    kv_grad = kv_grad.at[:, glob_local].add(glob_mine)
    collected = jnp.dot(
        onehot(asked_flat, table_rows).T, returned, preferred_element_type=jnp.float32
    ).reshape(block_rows, kv_dev, 2, BLK, HD)
    kv_grad = kv_grad + collected.transpose(2, 0, 3, 1, 4)

    attended = attended.reshape(tok_rows, kv_dev * GROUP * HD)
    query_grad = (
        unrotate(query_portion.reshape(tok_rows, kv_dev * GROUP, HD), cosines, sine_vals)
        .astype(jnp.bfloat16)
        .reshape(tok_rows, kv_dev * GROUP * HD)
    )
    key_acc = kv_grad[0].reshape(tok_rows, kv_dev, HD)
    key_grad = (
        unrotate(key_acc, cosines, sine_vals).astype(jnp.bfloat16).reshape(tok_rows, kv_dev * HD)
    )
    value_grad = kv_grad[1].reshape(tok_rows, kv_dev * HD).astype(jnp.bfloat16)
    return (attended, query_grad, key_grad, value_grad)


def solution(mesh):
    in_specs = (
        P("seq", "head"),
        P("seq", "head"),
        P("seq", "head"),
        P(None, "seq"),
        P("seq", "head", None),
        P(),
        P("seq", "head"),
    )
    out_specs = (P("seq", "head"), P("seq", "head"), P("seq", "head"), P("seq", "head"))
    return jax.shard_map(local, mesh=mesh, in_specs=in_specs, out_specs=out_specs, check_vma=False)
```

```python
import math

import jax
import jax.numpy as jnp
from jax import lax
from jax.sharding import PartitionSpec as P

HD = 128
GROUP = 4
BLK = 64
GLOB = 2
RND = 3


NEG_FILL = -1e30
ROPE_BASE = 1000000.0


def extended(array, sides, width):
    for axis, dim in sides:
        devices, length = (lax.axis_size(axis), array.shape[dim])
        up = [(i, (i + 1) % devices) for i in range(devices - 1)]
        down = [(j, i) for i, j in up]
        last = lax.slice_in_dim(array, length - width, length, axis=dim)
        leading = lax.slice_in_dim(array, 0, width, axis=dim)
        before = lax.ppermute(last, axis, up)
        after = lax.ppermute(leading, axis, down)
        array = jnp.concatenate([before, array, after], axis=dim)
    return array


def spread(block, axis, source):
    block = jnp.where(lax.axis_index(axis) == source, block, jnp.zeros_like(block))
    return lax.psum(block, axis)


def shifted(array, axis, by):
    devices = lax.axis_size(axis)
    pairs = [(i, i + by) for i in range(devices) if 0 <= i + by < devices]
    return lax.ppermute(array, axis, pairs)


def tables(positions):
    half_dim = HD // 2
    freq_ids = jnp.arange(half_dim)
    inv_freq = jnp.power(jnp.float32(ROPE_BASE), -2.0 * freq_ids.astype(jnp.float32) / HD)
    pos_float = positions.astype(jnp.float32)
    chosen = jnp.where(
        (freq_ids % 3 == 0)[None, :],
        pos_float[0][:, None],
        jnp.where((freq_ids % 3 == 1)[None, :], pos_float[1][:, None], pos_float[2][:, None]),
    )
    angles = chosen * inv_freq[None, :]
    return (jnp.cos(angles), jnp.sin(angles))


def rotate(states, cosines, sine_vals):
    half_dim = HD // 2
    first_half = states[..., :half_dim]
    second_half = states[..., half_dim:]
    cos_b = cosines[:, None, :]
    sin_b = sine_vals[:, None, :]
    return jnp.concatenate(
        [first_half * cos_b - second_half * sin_b, second_half * cos_b + first_half * sin_b],
        axis=-1,
    )


def unrotate(states, cosines, sine_vals):
    half_dim = HD // 2
    first_half = states[..., :half_dim]
    second_half = states[..., half_dim:]
    cos_b = cosines[:, None, :]
    sin_b = sine_vals[:, None, :]
    return jnp.concatenate(
        [first_half * cos_b + second_half * sin_b, second_half * cos_b - first_half * sin_b],
        axis=-1,
    )


def attend(query_block_view, key_block_view, value_block_view, gradient_block_view, key_mask):
    score_scale = 1.0 / math.sqrt(HD)
    logit_scores = (
        jnp.einsum(
            "mtyp,mop->myto", query_block_view, key_block_view, preferred_element_type=jnp.float32
        )
        * score_scale
    )
    logit_scores = jnp.where(key_mask[:, None, None, :], logit_scores, NEG_FILL)
    row_max = jnp.max(logit_scores, axis=-1, keepdims=True)
    exponent = jnp.exp(logit_scores - row_max)
    probability = exponent / jnp.sum(exponent, axis=-1, keepdims=True)
    attention_weights = probability.astype(jnp.bfloat16)
    attended = jnp.einsum(
        "ywiu,yuz->yiwz", attention_weights, value_block_view, preferred_element_type=jnp.float32
    ).astype(jnp.bfloat16)
    weight_gradient = jnp.einsum(
        "mtyp,mop->myto", gradient_block_view, value_block_view, preferred_element_type=jnp.float32
    )
    row_delta = jnp.sum(
        gradient_block_view.astype(jnp.float32) * attended.astype(jnp.float32), axis=-1
    )
    row_delta = jnp.transpose(row_delta, (0, 2, 1))[..., None]
    score_gradient = (probability * (weight_gradient - row_delta) * score_scale).astype(
        jnp.bfloat16
    )
    value_portion = jnp.einsum(
        "pcht,phca->pta", attention_weights, gradient_block_view, preferred_element_type=jnp.float32
    )
    key_portion = jnp.einsum(
        "pcht,phca->pta", score_gradient, query_block_view, preferred_element_type=jnp.float32
    )
    query_portion = jnp.einsum(
        "ywiu,yuz->yiwz", score_gradient, key_block_view, preferred_element_type=jnp.float32
    )
    return (attended, query_portion, key_portion, value_portion)


def onehot(ids, count):
    return (ids[:, None] == jnp.arange(count, dtype=jnp.int32)[None, :]).astype(jnp.bfloat16)


def exchange(array):
    return lax.all_to_all(array, "seq", 0, 0, tiled=True)


def local(queries, key_states, value_states, positions, random_blocks, global_blocks, out_grad):
    tok_rows = queries.shape[0]
    block_rows = tok_rows // BLK
    kv_dev = key_states.shape[1] // HD
    seq_count = lax.axis_size("seq")
    my_index = lax.axis_index("seq")
    slot_count = block_rows * kv_dev * RND
    capacity = (slot_count + seq_count - 1) // seq_count + 1
    score_scale = 1.0 / math.sqrt(HD)
    table_rows = block_rows * kv_dev
    piece = 2 * BLK * kv_dev * HD // seq_count
    code_cols = 128

    cosines, sine_vals = tables(positions)
    q_rot = rotate(
        queries.reshape(tok_rows, kv_dev * GROUP, HD).astype(jnp.float32), cosines, sine_vals
    ).astype(jnp.bfloat16)
    k_rot = rotate(
        key_states.reshape(tok_rows, kv_dev, HD).astype(jnp.float32), cosines, sine_vals
    ).astype(jnp.bfloat16)
    paired = jnp.stack([k_rot.reshape(tok_rows, kv_dev * HD), value_states])
    own_blocks = paired.reshape(2, block_rows, BLK, kv_dev, HD)

    flat_ids = random_blocks.reshape(slot_count)
    owners = flat_ids // block_rows
    head_ids = jnp.broadcast_to(
        jnp.arange(kv_dev, dtype=jnp.int32)[None, :, None], (block_rows, kv_dev, RND)
    ).reshape(slot_count)
    req_code = flat_ids % block_rows * kv_dev + head_ids
    slot_ids = jnp.arange(slot_count, dtype=jnp.int32)
    earlier = (owners[:, None] == owners[None, :]) & (slot_ids[None, :] < slot_ids[:, None])
    slot_pos = owners * capacity + jnp.sum(earlier, axis=1)
    request = jnp.zeros((seq_count * capacity,), jnp.int32).at[slot_pos].set(req_code)
    request = request.reshape(seq_count, capacity)
    glob_owner = global_blocks // block_rows
    glob_local = global_blocks % block_rows
    glob_scatter = []
    for which_glob in range(GLOB):
        glob_piece = lax.dynamic_index_in_dim(own_blocks, glob_local[which_glob], 1, keepdims=False)
        glob_piece = jnp.where(my_index == glob_owner[which_glob], glob_piece, jnp.zeros_like(glob_piece))
        glob_scatter.append(glob_piece.reshape(seq_count, piece))
    first_out = jnp.concatenate(
        glob_scatter
        + [request.astype(jnp.bfloat16), jnp.zeros((seq_count, code_cols - capacity), jnp.bfloat16)],
        axis=1,
    )
    first_in = exchange(first_out)
    asked_part = first_in[:, GLOB * piece : GLOB * piece + capacity].astype(jnp.int32)
    my_pieces = jnp.stack(
        [
            lax.dynamic_index_in_dim(first_in, glob_owner[g], 0, keepdims=False)[g * piece : (g + 1) * piece]
            for g in range(GLOB)
        ]
    )
    glob_in = exchange(jnp.broadcast_to(my_pieces[None], (seq_count, GLOB, piece)))
    glob_kv = glob_in.transpose(1, 0, 2).reshape(GLOB, 2, BLK, kv_dev, HD).transpose(1, 0, 2, 3, 4)

    kv_table = own_blocks.transpose(1, 3, 0, 2, 4).reshape(table_rows, 2, BLK, HD)
    asked_flat = asked_part.reshape(seq_count * capacity)
    answers = jnp.einsum(
        "sq,qkte->skte", onehot(asked_flat, table_rows), kv_table, preferred_element_type=jnp.float32
    ).astype(jnp.bfloat16)
    padded = extended(paired, (("seq", 1),), BLK)
    answers, padded, glob_kv = lax.optimization_barrier((answers, padded, glob_kv))
    window_blocks = padded.reshape(2, block_rows + 2, BLK, kv_dev, HD)
    fetched = exchange(answers.reshape(seq_count, capacity, 2, BLK, HD)).reshape(
        seq_count * capacity, 2, BLK, HD
    )

    window_set = jnp.stack([window_blocks[:, offset : offset + block_rows] for offset in range(3)], axis=2)
    glob_set = jnp.broadcast_to(glob_kv[:, None], (2, block_rows, GLOB, BLK, kv_dev, HD))
    near_set = jnp.concatenate([window_set, glob_set], axis=2).reshape(
        2, block_rows, (3 + GLOB) * BLK, kv_dev, HD
    )
    window_ids = (
        my_index * block_rows + jnp.arange(block_rows)[:, None] + jnp.arange(-1, 2)[None, :]
    )
    window_ok = (window_ids >= 0) & (window_ids < seq_count * block_rows)
    near_ok = jnp.concatenate([window_ok, jnp.ones((block_rows, GLOB), dtype=bool)], axis=1)
    near_mask = jnp.repeat(near_ok, BLK, axis=1)

    query_nat = q_rot.reshape(block_rows, BLK, kv_dev, GROUP, HD)
    grad_nat = out_grad.reshape(block_rows, BLK, kv_dev, GROUP, HD)
    near_k = near_set[0]
    near_v = near_set[1]
    near_scores = (
        jnp.einsum("rthgd,rkhd->rhgtk", query_nat, near_k, preferred_element_type=jnp.float32)
        * score_scale
    )
    near_scores = jnp.where(near_mask[:, None, None, None, :], near_scores, NEG_FILL)
    near_wgrad = jnp.einsum("rthgd,rkhd->rhgtk", grad_nat, near_v, preferred_element_type=jnp.float32)

    random_kv = fetched[slot_pos].reshape(block_rows, kv_dev, RND, 2, BLK, HD)
    far_k = random_kv[:, :, :, 0].reshape(block_rows, kv_dev, RND * BLK, HD)
    far_v = random_kv[:, :, :, 1].reshape(block_rows, kv_dev, RND * BLK, HD)
    far_scores = (
        jnp.einsum("rthgd,rhkd->rhgtk", query_nat, far_k, preferred_element_type=jnp.float32)
        * score_scale
    )
    far_wgrad = jnp.einsum("rthgd,rhkd->rhgtk", grad_nat, far_v, preferred_element_type=jnp.float32)
    row_max = jnp.maximum(
        jnp.max(near_scores, axis=-1, keepdims=True), jnp.max(far_scores, axis=-1, keepdims=True)
    )
    near_exp = jnp.exp(near_scores - row_max)
    far_exp = jnp.exp(far_scores - row_max)
    total = jnp.sum(near_exp, axis=-1, keepdims=True) + jnp.sum(far_exp, axis=-1, keepdims=True)
    near_prob = near_exp / total
    far_prob = far_exp / total
    near_w = near_prob.astype(jnp.bfloat16)
    far_w = far_prob.astype(jnp.bfloat16)
    attended = (
        jnp.einsum("rhgtk,rkhd->rthgd", near_w, near_v, preferred_element_type=jnp.float32)
        + jnp.einsum("rhgtk,rhkd->rthgd", far_w, far_v, preferred_element_type=jnp.float32)
    ).astype(jnp.bfloat16)
    row_delta = jnp.sum(grad_nat.astype(jnp.float32) * attended.astype(jnp.float32), axis=-1)
    row_delta = row_delta.transpose(0, 2, 3, 1)[..., None]
    near_sgrad = (near_prob * (near_wgrad - row_delta) * score_scale).astype(jnp.bfloat16)
    far_sgrad = (far_prob * (far_wgrad - row_delta) * score_scale).astype(jnp.bfloat16)

    far_kgrad = jnp.einsum("rhgtk,rthgd->rhkd", far_sgrad, query_nat, preferred_element_type=jnp.float32)
    far_vgrad = jnp.einsum("rhgtk,rthgd->rhkd", far_w, grad_nat, preferred_element_type=jnp.float32)
    random_grad = jnp.stack(
        [
            far_kgrad.reshape(block_rows, kv_dev, RND, BLK, HD),
            far_vgrad.reshape(block_rows, kv_dev, RND, BLK, HD),
        ],
        axis=3,
    ).reshape(slot_count, 2, BLK, HD).astype(jnp.bfloat16)
    outgoing = jnp.einsum(
        "ps,pkte->skte",
        onehot(slot_pos, seq_count * capacity),
        random_grad,
        preferred_element_type=jnp.float32,
    ).astype(jnp.bfloat16)
    query_portion = jnp.einsum(
        "rhgtk,rkhd->rthgd", near_sgrad, near_k, preferred_element_type=jnp.float32
    ) + jnp.einsum("rhgtk,rhkd->rthgd", far_sgrad, far_k, preferred_element_type=jnp.float32)
    near_kgrad = jnp.einsum("rhgtk,rthgd->rkhd", near_sgrad, query_nat, preferred_element_type=jnp.float32)
    near_vgrad = jnp.einsum("rhgtk,rthgd->rkhd", near_w, grad_nat, preferred_element_type=jnp.float32)
    near_grad = jnp.stack([near_kgrad, near_vgrad]).reshape(2, block_rows, 3 + GLOB, BLK, kv_dev, HD)
    window_acc = jnp.pad(near_grad[:, :, 0], ((0, 0), (0, 2), (0, 0), (0, 0), (0, 0)))
    window_acc = window_acc + jnp.pad(near_grad[:, :, 1], ((0, 0), (1, 1), (0, 0), (0, 0), (0, 0)))
    window_acc = window_acc + jnp.pad(near_grad[:, :, 2], ((0, 0), (2, 0), (0, 0), (0, 0), (0, 0)))
    from_right = shifted(window_acc[:, 0].astype(jnp.bfloat16), "seq", -1).astype(jnp.float32)
    from_left = shifted(window_acc[:, block_rows + 1].astype(jnp.bfloat16), "seq", 1).astype(jnp.float32)
    glob_local_grad = jnp.sum(near_grad[:, :, 3:], axis=1)
    glob_split = glob_local_grad.transpose(1, 0, 2, 3, 4).reshape(GLOB, seq_count, piece)
    piece_sum = jnp.sum(exchange(glob_split.transpose(1, 0, 2)), axis=0)
    to_owner = jnp.where(
        jnp.arange(seq_count)[:, None, None] == glob_owner[None, :, None], piece_sum[None], 0.0
    )
    glob_grad = exchange(to_owner).transpose(1, 0, 2).reshape(GLOB, 2, BLK, kv_dev, HD)
    outgoing, from_right, from_left, glob_grad = lax.optimization_barrier(
        (outgoing, from_right, from_left, glob_grad)
    )
    returned = exchange(outgoing.reshape(seq_count, capacity, 2, BLK, HD)).reshape(
        seq_count * capacity, 2, BLK, HD
    )

    kv_grad = window_acc[:, 1 : block_rows + 1]
    kv_grad = kv_grad.at[:, block_rows - 1].add(from_right).at[:, 0].add(from_left)
    glob_mine = jnp.where((glob_owner == my_index)[:, None, None, None, None], glob_grad, 0.0)
    kv_grad = kv_grad.at[:, glob_local].add(glob_mine.transpose(1, 0, 2, 3, 4))
    collected = jnp.einsum(
        "sq,skte->qkte", onehot(asked_flat, table_rows), returned, preferred_element_type=jnp.float32
    ).reshape(block_rows, kv_dev, 2, BLK, HD)
    kv_grad = kv_grad + collected.transpose(2, 0, 3, 1, 4)

    attended = attended.reshape(tok_rows, kv_dev * GROUP * HD)
    query_grad = (
        unrotate(query_portion.reshape(tok_rows, kv_dev * GROUP, HD), cosines, sine_vals)
        .astype(jnp.bfloat16)
        .reshape(tok_rows, kv_dev * GROUP * HD)
    )
    key_acc = kv_grad[0].reshape(tok_rows, kv_dev, HD)
    key_grad = (
        unrotate(key_acc, cosines, sine_vals).astype(jnp.bfloat16).reshape(tok_rows, kv_dev * HD)
    )
    value_grad = kv_grad[1].reshape(tok_rows, kv_dev * HD).astype(jnp.bfloat16)
    return (attended, query_grad, key_grad, value_grad)


def solution(mesh):
    in_specs = (
        P("seq", "head"),
        P("seq", "head"),
        P("seq", "head"),
        P(None, "seq"),
        P("seq", "head", None),
        P(),
        P("seq", "head"),
    )
    out_specs = (P("seq", "head"), P("seq", "head"), P("seq", "head"), P("seq", "head"))
    return jax.shard_map(local, mesh=mesh, in_specs=in_specs, out_specs=out_specs, check_vma=False)
```

```python
import math

import jax
import jax.numpy as jnp
from jax import lax
from jax.sharding import PartitionSpec as P

HD = 128
GROUP = 4
BLK = 64
GLOB = 2
RND = 3


NEG_FILL = -1e30
ROPE_BASE = 1000000.0


def extended(array, sides, width):
    for axis, dim in sides:
        devices, length = (lax.axis_size(axis), array.shape[dim])
        up = [(i, (i + 1) % devices) for i in range(devices - 1)]
        down = [(j, i) for i, j in up]
        last = lax.slice_in_dim(array, length - width, length, axis=dim)
        leading = lax.slice_in_dim(array, 0, width, axis=dim)
        before = lax.ppermute(last, axis, up)
        after = lax.ppermute(leading, axis, down)
        array = jnp.concatenate([before, array, after], axis=dim)
    return array


def spread(block, axis, source):
    block = jnp.where(lax.axis_index(axis) == source, block, jnp.zeros_like(block))
    return lax.psum(block, axis)


def shifted(array, axis, by):
    devices = lax.axis_size(axis)
    pairs = [(i, i + by) for i in range(devices) if 0 <= i + by < devices]
    return lax.ppermute(array, axis, pairs)


def tables(positions):
    half_dim = HD // 2
    freq_ids = jnp.arange(half_dim)
    inv_freq = jnp.power(jnp.float32(ROPE_BASE), -2.0 * freq_ids.astype(jnp.float32) / HD)
    pos_float = positions.astype(jnp.float32)
    chosen = jnp.where(
        (freq_ids % 3 == 0)[None, :],
        pos_float[0][:, None],
        jnp.where((freq_ids % 3 == 1)[None, :], pos_float[1][:, None], pos_float[2][:, None]),
    )
    angles = chosen * inv_freq[None, :]
    return (jnp.cos(angles), jnp.sin(angles))


def rotate(states, cosines, sine_vals):
    half_dim = HD // 2
    first_half = states[..., :half_dim]
    second_half = states[..., half_dim:]
    cos_b = cosines[:, None, :]
    sin_b = sine_vals[:, None, :]
    return jnp.concatenate(
        [first_half * cos_b - second_half * sin_b, second_half * cos_b + first_half * sin_b],
        axis=-1,
    )


def unrotate(states, cosines, sine_vals):
    half_dim = HD // 2
    first_half = states[..., :half_dim]
    second_half = states[..., half_dim:]
    cos_b = cosines[:, None, :]
    sin_b = sine_vals[:, None, :]
    return jnp.concatenate(
        [first_half * cos_b + second_half * sin_b, second_half * cos_b - first_half * sin_b],
        axis=-1,
    )


def attend(query_block_view, key_block_view, value_block_view, gradient_block_view, key_mask):
    score_scale = 1.0 / math.sqrt(HD)
    logit_scores = (
        jnp.einsum(
            "mtyp,mop->myto", query_block_view, key_block_view, preferred_element_type=jnp.float32
        )
        * score_scale
    )
    logit_scores = jnp.where(key_mask[:, None, None, :], logit_scores, NEG_FILL)
    row_max = jnp.max(logit_scores, axis=-1, keepdims=True)
    exponent = jnp.exp(logit_scores - row_max)
    probability = exponent / jnp.sum(exponent, axis=-1, keepdims=True)
    attention_weights = probability.astype(jnp.bfloat16)
    attended = jnp.einsum(
        "ywiu,yuz->yiwz", attention_weights, value_block_view, preferred_element_type=jnp.float32
    ).astype(jnp.bfloat16)
    weight_gradient = jnp.einsum(
        "mtyp,mop->myto", gradient_block_view, value_block_view, preferred_element_type=jnp.float32
    )
    row_delta = jnp.sum(
        gradient_block_view.astype(jnp.float32) * attended.astype(jnp.float32), axis=-1
    )
    row_delta = jnp.transpose(row_delta, (0, 2, 1))[..., None]
    score_gradient = (probability * (weight_gradient - row_delta) * score_scale).astype(
        jnp.bfloat16
    )
    value_portion = jnp.einsum(
        "pcht,phca->pta", attention_weights, gradient_block_view, preferred_element_type=jnp.float32
    )
    key_portion = jnp.einsum(
        "pcht,phca->pta", score_gradient, query_block_view, preferred_element_type=jnp.float32
    )
    query_portion = jnp.einsum(
        "ywiu,yuz->yiwz", score_gradient, key_block_view, preferred_element_type=jnp.float32
    )
    return (attended, query_portion, key_portion, value_portion)


def onehot(ids, count):
    return (ids[:, None] == jnp.arange(count, dtype=jnp.int32)[None, :]).astype(jnp.bfloat16)


def exchange(array):
    return lax.all_to_all(array, "seq", 0, 0, tiled=True)


def pick(ids, table):
    return jnp.einsum(
        "sq,qte->ste", onehot(ids, table.shape[0]), table, preferred_element_type=jnp.float32
    )


def local(queries, key_states, value_states, positions, random_blocks, global_blocks, out_grad):
    tok_rows = queries.shape[0]
    block_rows = tok_rows // BLK
    kv_dev = key_states.shape[1] // HD
    seq_count = lax.axis_size("seq")
    my_index = lax.axis_index("seq")
    slot_count = block_rows * kv_dev * RND
    capacity = (slot_count + seq_count - 1) // seq_count + 1
    score_scale = 1.0 / math.sqrt(HD)
    table_rows = block_rows * kv_dev
    piece = 2 * BLK * kv_dev * HD // seq_count
    glob_rows = GLOB * piece // HD
    code_cols = 128

    cosines, sine_vals = tables(positions)
    q_rot = rotate(
        queries.reshape(tok_rows, kv_dev * GROUP, HD).astype(jnp.float32), cosines, sine_vals
    ).astype(jnp.bfloat16)
    k_rot = rotate(
        key_states.reshape(tok_rows, kv_dev, HD).astype(jnp.float32), cosines, sine_vals
    ).astype(jnp.bfloat16)
    paired = jnp.stack([k_rot.reshape(tok_rows, kv_dev * HD), value_states])
    own_blocks = paired.reshape(2, block_rows, BLK, kv_dev, HD)

    flat_ids = random_blocks.reshape(slot_count)
    owners = flat_ids // block_rows
    head_ids = jnp.broadcast_to(
        jnp.arange(kv_dev, dtype=jnp.int32)[None, :, None], (block_rows, kv_dev, RND)
    ).reshape(slot_count)
    req_code = flat_ids % block_rows * kv_dev + head_ids
    slot_ids = jnp.arange(slot_count, dtype=jnp.int32)
    earlier = (owners[:, None] == owners[None, :]) & (slot_ids[None, :] < slot_ids[:, None])
    slot_pos = owners * capacity + jnp.sum(earlier, axis=1)
    request = jnp.zeros((seq_count * capacity,), jnp.int32).at[slot_pos].set(req_code)
    request = request.reshape(seq_count, capacity)
    glob_owner = global_blocks // block_rows
    glob_local = global_blocks % block_rows
    glob_scatter = []
    for which_glob in range(GLOB):
        glob_piece = lax.dynamic_index_in_dim(own_blocks, glob_local[which_glob], 1, keepdims=False)
        glob_piece = jnp.where(my_index == glob_owner[which_glob], glob_piece, jnp.zeros_like(glob_piece))
        glob_scatter.append(glob_piece.reshape(seq_count, piece))
    first_out = jnp.concatenate(
        glob_scatter
        + [request.astype(jnp.bfloat16), jnp.zeros((seq_count, code_cols - capacity), jnp.bfloat16)],
        axis=1,
    )
    first_in = exchange(first_out)
    asked_part = first_in[:, GLOB * piece : GLOB * piece + capacity].astype(jnp.int32)
    my_pieces = jnp.concatenate(
        [
            lax.dynamic_index_in_dim(first_in, glob_owner[g], 0, keepdims=False)[g * piece : (g + 1) * piece]
            for g in range(GLOB)
        ]
    )
    asked_flat = asked_part.reshape(seq_count * capacity)

    k_table = own_blocks[0].transpose(0, 2, 1, 3).reshape(table_rows, BLK, HD)
    v_table = own_blocks[1].transpose(0, 2, 1, 3).reshape(table_rows, BLK, HD)
    answers_k = pick(asked_flat, k_table).astype(jnp.bfloat16).reshape(seq_count, capacity * BLK, HD)
    answers_k = jnp.concatenate(
        [answers_k, jnp.broadcast_to(my_pieces.reshape(1, glob_rows, HD), (seq_count, glob_rows, HD))],
        axis=1,
    )
    answers_v = pick(asked_flat, v_table).astype(jnp.bfloat16).reshape(seq_count, capacity * BLK, HD)
    padded = extended(paired, (("seq", 1),), BLK)
    answers_k, padded = lax.optimization_barrier((answers_k, padded))
    fetched_k = exchange(answers_k)
    answers_v, fetched_k = lax.optimization_barrier((answers_v, fetched_k))
    fetched_v = exchange(answers_v).reshape(seq_count * capacity, BLK, HD)
    glob_in = fetched_k[:, capacity * BLK :].reshape(seq_count, GLOB, piece)
    fetched_k = fetched_k[:, : capacity * BLK].reshape(seq_count * capacity, BLK, HD)
    glob_kv = glob_in.transpose(1, 0, 2).reshape(GLOB, 2, BLK, kv_dev, HD).transpose(1, 0, 2, 3, 4)

    window_blocks = padded.reshape(2, block_rows + 2, BLK, kv_dev, HD)
    window_set = jnp.stack([window_blocks[:, offset : offset + block_rows] for offset in range(3)], axis=2)
    glob_set = jnp.broadcast_to(glob_kv[:, None], (2, block_rows, GLOB, BLK, kv_dev, HD))
    near_set = jnp.concatenate([window_set, glob_set], axis=2).reshape(
        2, block_rows, (3 + GLOB) * BLK, kv_dev, HD
    )
    window_ids = (
        my_index * block_rows + jnp.arange(block_rows)[:, None] + jnp.arange(-1, 2)[None, :]
    )
    window_ok = (window_ids >= 0) & (window_ids < seq_count * block_rows)
    near_ok = jnp.concatenate([window_ok, jnp.ones((block_rows, GLOB), dtype=bool)], axis=1)
    near_mask = jnp.repeat(near_ok, BLK, axis=1)

    query_nat = q_rot.reshape(block_rows, BLK, kv_dev, GROUP, HD)
    grad_nat = out_grad.reshape(block_rows, BLK, kv_dev, GROUP, HD)
    near_k = near_set[0]
    near_v = near_set[1]
    far_k = fetched_k[slot_pos].reshape(block_rows, kv_dev, RND * BLK, HD)
    far_v = fetched_v[slot_pos].reshape(block_rows, kv_dev, RND * BLK, HD)
    near_scores = (
        jnp.einsum("rthgd,rkhd->rhgtk", query_nat, near_k, preferred_element_type=jnp.float32)
        * score_scale
    )
    near_scores = jnp.where(near_mask[:, None, None, None, :], near_scores, NEG_FILL)
    far_scores = (
        jnp.einsum("rthgd,rhkd->rhgtk", query_nat, far_k, preferred_element_type=jnp.float32)
        * score_scale
    )
    row_max = jnp.maximum(
        jnp.max(near_scores, axis=-1, keepdims=True), jnp.max(far_scores, axis=-1, keepdims=True)
    )
    near_exp = jnp.exp(near_scores - row_max)
    far_exp = jnp.exp(far_scores - row_max)
    total = jnp.sum(near_exp, axis=-1, keepdims=True) + jnp.sum(far_exp, axis=-1, keepdims=True)
    near_prob = near_exp / total
    far_prob = far_exp / total
    near_w = near_prob.astype(jnp.bfloat16)
    far_w = far_prob.astype(jnp.bfloat16)

    far_vgrad = jnp.einsum("rhgtk,rthgd->rhkd", far_w, grad_nat, preferred_element_type=jnp.float32)
    out_v = jnp.einsum(
        "ps,pte->ste",
        onehot(slot_pos, seq_count * capacity),
        far_vgrad.astype(jnp.bfloat16).reshape(slot_count, BLK, HD),
        preferred_element_type=jnp.float32,
    ).astype(jnp.bfloat16)
    returned_v = exchange(out_v.reshape(seq_count, capacity * BLK, HD)).reshape(
        seq_count * capacity, BLK, HD
    )

    near_wgrad = jnp.einsum("rthgd,rkhd->rhgtk", grad_nat, near_v, preferred_element_type=jnp.float32)
    far_wgrad = jnp.einsum("rthgd,rhkd->rhgtk", grad_nat, far_v, preferred_element_type=jnp.float32)
    attended = (
        jnp.einsum("rhgtk,rkhd->rthgd", near_w, near_v, preferred_element_type=jnp.float32)
        + jnp.einsum("rhgtk,rhkd->rthgd", far_w, far_v, preferred_element_type=jnp.float32)
    ).astype(jnp.bfloat16)
    row_delta = jnp.sum(grad_nat.astype(jnp.float32) * attended.astype(jnp.float32), axis=-1)
    row_delta = row_delta.transpose(0, 2, 3, 1)[..., None]
    near_sgrad = (near_prob * (near_wgrad - row_delta) * score_scale).astype(jnp.bfloat16)
    far_sgrad = (far_prob * (far_wgrad - row_delta) * score_scale).astype(jnp.bfloat16)

    far_kgrad = jnp.einsum("rhgtk,rthgd->rhkd", far_sgrad, query_nat, preferred_element_type=jnp.float32)
    out_k = jnp.einsum(
        "ps,pte->ste",
        onehot(slot_pos, seq_count * capacity),
        far_kgrad.astype(jnp.bfloat16).reshape(slot_count, BLK, HD),
        preferred_element_type=jnp.float32,
    ).astype(jnp.bfloat16).reshape(seq_count, capacity * BLK, HD)
    near_kgrad = jnp.einsum("rhgtk,rthgd->rkhd", near_sgrad, query_nat, preferred_element_type=jnp.float32)
    near_vgrad = jnp.einsum("rhgtk,rthgd->rkhd", near_w, grad_nat, preferred_element_type=jnp.float32)
    near_grad = jnp.stack([near_kgrad, near_vgrad]).reshape(2, block_rows, 3 + GLOB, BLK, kv_dev, HD)
    glob_local_grad = jnp.sum(near_grad[:, :, 3:], axis=1)
    glob_split = glob_local_grad.transpose(1, 0, 2, 3, 4).reshape(GLOB, seq_count, piece)
    glob_split = glob_split.transpose(1, 0, 2).reshape(seq_count, glob_rows, HD)
    glob_high = glob_split.astype(jnp.bfloat16)
    glob_low = (glob_split - glob_high.astype(jnp.float32)).astype(jnp.bfloat16)
    returned_k = exchange(jnp.concatenate([out_k, glob_high, glob_low], axis=1))
    glob_back = returned_k[:, capacity * BLK :].astype(jnp.float32)
    piece_sum = jnp.sum(glob_back[:, :glob_rows] + glob_back[:, glob_rows:], axis=0).reshape(GLOB, piece)
    returned_k = returned_k[:, : capacity * BLK].reshape(seq_count * capacity, BLK, HD)
    to_owner = jnp.where(
        jnp.arange(seq_count)[:, None, None] == glob_owner[None, :, None], piece_sum[None], 0.0
    )
    glob_grad = exchange(to_owner).transpose(1, 0, 2).reshape(GLOB, 2, BLK, kv_dev, HD)

    query_portion = jnp.einsum(
        "rhgtk,rkhd->rthgd", near_sgrad, near_k, preferred_element_type=jnp.float32
    ) + jnp.einsum("rhgtk,rhkd->rthgd", far_sgrad, far_k, preferred_element_type=jnp.float32)
    window_acc = jnp.pad(near_grad[:, :, 0], ((0, 0), (0, 2), (0, 0), (0, 0), (0, 0)))
    window_acc = window_acc + jnp.pad(near_grad[:, :, 1], ((0, 0), (1, 1), (0, 0), (0, 0), (0, 0)))
    window_acc = window_acc + jnp.pad(near_grad[:, :, 2], ((0, 0), (2, 0), (0, 0), (0, 0), (0, 0)))
    from_right = shifted(window_acc[:, 0].astype(jnp.bfloat16), "seq", -1).astype(jnp.float32)
    from_left = shifted(window_acc[:, block_rows + 1].astype(jnp.bfloat16), "seq", 1).astype(jnp.float32)

    kv_grad = window_acc[:, 1 : block_rows + 1]
    kv_grad = kv_grad.at[:, block_rows - 1].add(from_right).at[:, 0].add(from_left)
    glob_mine = jnp.where((glob_owner == my_index)[:, None, None, None, None], glob_grad, 0.0)
    kv_grad = kv_grad.at[:, glob_local].add(glob_mine.transpose(1, 0, 2, 3, 4))
    oh_back = onehot(asked_flat, table_rows).T
    collected = jnp.stack(
        [
            jnp.einsum("qs,ste->qte", oh_back, returned_k, preferred_element_type=jnp.float32),
            jnp.einsum("qs,ste->qte", oh_back, returned_v, preferred_element_type=jnp.float32),
        ]
    ).reshape(2, block_rows, kv_dev, BLK, HD)
    kv_grad = kv_grad + collected.transpose(0, 1, 3, 2, 4)

    attended = attended.reshape(tok_rows, kv_dev * GROUP * HD)
    query_grad = (
        unrotate(query_portion.reshape(tok_rows, kv_dev * GROUP, HD), cosines, sine_vals)
        .astype(jnp.bfloat16)
        .reshape(tok_rows, kv_dev * GROUP * HD)
    )
    key_acc = kv_grad[0].reshape(tok_rows, kv_dev, HD)
    key_grad = (
        unrotate(key_acc, cosines, sine_vals).astype(jnp.bfloat16).reshape(tok_rows, kv_dev * HD)
    )
    value_grad = kv_grad[1].reshape(tok_rows, kv_dev * HD).astype(jnp.bfloat16)
    return (attended, query_grad, key_grad, value_grad)


def solution(mesh):
    in_specs = (
        P("seq", "head"),
        P("seq", "head"),
        P("seq", "head"),
        P(None, "seq"),
        P("seq", "head", None),
        P(),
        P("seq", "head"),
    )
    out_specs = (P("seq", "head"), P("seq", "head"), P("seq", "head"), P("seq", "head"))
    return jax.shard_map(local, mesh=mesh, in_specs=in_specs, out_specs=out_specs, check_vma=False)
```

```python
import math

import jax
import jax.numpy as jnp
from jax import lax
from jax.sharding import PartitionSpec as P

HD = 128
GROUP = 4
BLK = 64
GLOB = 2
RND = 3


NEG_FILL = -1e30
ROPE_BASE = 1000000.0


def extended(array, sides, width):
    for axis, dim in sides:
        devices, length = (lax.axis_size(axis), array.shape[dim])
        up = [(i, (i + 1) % devices) for i in range(devices - 1)]
        down = [(j, i) for i, j in up]
        last = lax.slice_in_dim(array, length - width, length, axis=dim)
        leading = lax.slice_in_dim(array, 0, width, axis=dim)
        before = lax.ppermute(last, axis, up)
        after = lax.ppermute(leading, axis, down)
        array = jnp.concatenate([before, array, after], axis=dim)
    return array


def spread(block, axis, source):
    block = jnp.where(lax.axis_index(axis) == source, block, jnp.zeros_like(block))
    return lax.psum(block, axis)


def shifted(array, axis, by):
    devices = lax.axis_size(axis)
    pairs = [(i, i + by) for i in range(devices) if 0 <= i + by < devices]
    return lax.ppermute(array, axis, pairs)


def tables(positions):
    half_dim = HD // 2
    freq_ids = jnp.arange(half_dim)
    inv_freq = jnp.power(jnp.float32(ROPE_BASE), -2.0 * freq_ids.astype(jnp.float32) / HD)
    pos_float = positions.astype(jnp.float32)
    chosen = jnp.where(
        (freq_ids % 3 == 0)[None, :],
        pos_float[0][:, None],
        jnp.where((freq_ids % 3 == 1)[None, :], pos_float[1][:, None], pos_float[2][:, None]),
    )
    angles = chosen * inv_freq[None, :]
    return (jnp.cos(angles), jnp.sin(angles))


def rotate(states, cosines, sine_vals):
    half_dim = HD // 2
    first_half = states[..., :half_dim]
    second_half = states[..., half_dim:]
    cos_b = cosines[:, None, :]
    sin_b = sine_vals[:, None, :]
    return jnp.concatenate(
        [first_half * cos_b - second_half * sin_b, second_half * cos_b + first_half * sin_b],
        axis=-1,
    )


def unrotate(states, cosines, sine_vals):
    half_dim = HD // 2
    first_half = states[..., :half_dim]
    second_half = states[..., half_dim:]
    cos_b = cosines[:, None, :]
    sin_b = sine_vals[:, None, :]
    return jnp.concatenate(
        [first_half * cos_b + second_half * sin_b, second_half * cos_b - first_half * sin_b],
        axis=-1,
    )


def attend(query_block_view, key_block_view, value_block_view, gradient_block_view, key_mask):
    score_scale = 1.0 / math.sqrt(HD)
    logit_scores = (
        jnp.einsum(
            "mtyp,mop->myto", query_block_view, key_block_view, preferred_element_type=jnp.float32
        )
        * score_scale
    )
    logit_scores = jnp.where(key_mask[:, None, None, :], logit_scores, NEG_FILL)
    row_max = jnp.max(logit_scores, axis=-1, keepdims=True)
    exponent = jnp.exp(logit_scores - row_max)
    probability = exponent / jnp.sum(exponent, axis=-1, keepdims=True)
    attention_weights = probability.astype(jnp.bfloat16)
    attended = jnp.einsum(
        "ywiu,yuz->yiwz", attention_weights, value_block_view, preferred_element_type=jnp.float32
    ).astype(jnp.bfloat16)
    weight_gradient = jnp.einsum(
        "mtyp,mop->myto", gradient_block_view, value_block_view, preferred_element_type=jnp.float32
    )
    row_delta = jnp.sum(
        gradient_block_view.astype(jnp.float32) * attended.astype(jnp.float32), axis=-1
    )
    row_delta = jnp.transpose(row_delta, (0, 2, 1))[..., None]
    score_gradient = (probability * (weight_gradient - row_delta) * score_scale).astype(
        jnp.bfloat16
    )
    value_portion = jnp.einsum(
        "pcht,phca->pta", attention_weights, gradient_block_view, preferred_element_type=jnp.float32
    )
    key_portion = jnp.einsum(
        "pcht,phca->pta", score_gradient, query_block_view, preferred_element_type=jnp.float32
    )
    query_portion = jnp.einsum(
        "ywiu,yuz->yiwz", score_gradient, key_block_view, preferred_element_type=jnp.float32
    )
    return (attended, query_portion, key_portion, value_portion)


def onehot(ids, count):
    return (ids[:, None] == jnp.arange(count, dtype=jnp.int32)[None, :]).astype(jnp.bfloat16)


def exchange(array):
    return lax.all_to_all(array, "seq", 0, 0, tiled=True)


def pick(ids, table):
    return jnp.einsum(
        "sq,qte->ste", onehot(ids, table.shape[0]), table, preferred_element_type=jnp.float32
    )


def local(queries, key_states, value_states, positions, random_blocks, global_blocks, out_grad):
    tok_rows = queries.shape[0]
    block_rows = tok_rows // BLK
    kv_dev = key_states.shape[1] // HD
    seq_count = lax.axis_size("seq")
    my_index = lax.axis_index("seq")
    slot_count = block_rows * kv_dev * RND
    capacity = (slot_count + seq_count - 1) // seq_count + 1
    score_scale = 1.0 / math.sqrt(HD)
    table_rows = block_rows * kv_dev
    piece = 2 * BLK * kv_dev * HD // seq_count
    glob_rows = GLOB * piece // HD
    code_cols = 128

    cosines, sine_vals = tables(positions)
    q_rot = rotate(
        queries.reshape(tok_rows, kv_dev * GROUP, HD).astype(jnp.float32), cosines, sine_vals
    ).astype(jnp.bfloat16)
    k_rot = rotate(
        key_states.reshape(tok_rows, kv_dev, HD).astype(jnp.float32), cosines, sine_vals
    ).astype(jnp.bfloat16)
    paired = jnp.stack([k_rot.reshape(tok_rows, kv_dev * HD), value_states])
    own_blocks = paired.reshape(2, block_rows, BLK, kv_dev, HD)

    flat_ids = random_blocks.reshape(slot_count)
    owners = flat_ids // block_rows
    head_ids = jnp.broadcast_to(
        jnp.arange(kv_dev, dtype=jnp.int32)[None, :, None], (block_rows, kv_dev, RND)
    ).reshape(slot_count)
    req_code = flat_ids % block_rows * kv_dev + head_ids
    slot_ids = jnp.arange(slot_count, dtype=jnp.int32)
    earlier = (owners[:, None] == owners[None, :]) & (slot_ids[None, :] < slot_ids[:, None])
    slot_pos = owners * capacity + jnp.sum(earlier, axis=1)
    request = jnp.zeros((seq_count * capacity,), jnp.int32).at[slot_pos].set(req_code)
    request = request.reshape(seq_count, capacity)
    glob_owner = global_blocks // block_rows
    glob_local = global_blocks % block_rows
    glob_scatter = []
    glob_cos, glob_sin = [], []
    for which_glob in range(GLOB):
        start = glob_local[which_glob] * BLK
        block_cos, block_sin = tables(lax.dynamic_slice_in_dim(positions, start, BLK, 1))
        glob_cos.append(block_cos)
        glob_sin.append(block_sin)
        block_keys = lax.dynamic_slice_in_dim(key_states, start, BLK, 0)
        block_keys = rotate(
            block_keys.reshape(BLK, kv_dev, HD).astype(jnp.float32), block_cos, block_sin
        ).astype(jnp.bfloat16)
        block_values = lax.dynamic_slice_in_dim(value_states, start, BLK, 0).reshape(BLK, kv_dev, HD)
        glob_piece = jnp.stack([block_keys, block_values])
        glob_piece = jnp.where(my_index == glob_owner[which_glob], glob_piece, jnp.zeros_like(glob_piece))
        glob_scatter.append(glob_piece.reshape(seq_count, piece))
    first_out = jnp.concatenate(
        glob_scatter
        + [request.astype(jnp.bfloat16), jnp.zeros((seq_count, code_cols - capacity), jnp.bfloat16)],
        axis=1,
    )
    first_in = exchange(first_out)
    asked_part = first_in[:, GLOB * piece : GLOB * piece + capacity].astype(jnp.int32)
    my_pieces = jnp.concatenate(
        [
            lax.dynamic_index_in_dim(first_in, glob_owner[g], 0, keepdims=False)[g * piece : (g + 1) * piece]
            for g in range(GLOB)
        ]
    )
    asked_flat = asked_part.reshape(seq_count * capacity)

    k_table = own_blocks[0].transpose(0, 2, 1, 3).reshape(table_rows, BLK, HD)
    v_table = own_blocks[1].transpose(0, 2, 1, 3).reshape(table_rows, BLK, HD)
    answers_k = pick(asked_flat, k_table).astype(jnp.bfloat16).reshape(seq_count, capacity * BLK, HD)
    answers_k = jnp.concatenate(
        [answers_k, jnp.broadcast_to(my_pieces.reshape(1, glob_rows, HD), (seq_count, glob_rows, HD))],
        axis=1,
    )
    answers_v = pick(asked_flat, v_table).astype(jnp.bfloat16).reshape(seq_count, capacity * BLK, HD)
    padded = extended(paired, (("seq", 1),), BLK)
    answers_k, padded = lax.optimization_barrier((answers_k, padded))
    fetched_k = exchange(answers_k)
    answers_v, fetched_k = lax.optimization_barrier((answers_v, fetched_k))
    fetched_v = exchange(answers_v).reshape(seq_count * capacity, BLK, HD)
    glob_in = fetched_k[:, capacity * BLK :].reshape(seq_count, GLOB, piece)
    fetched_k = fetched_k[:, : capacity * BLK].reshape(seq_count * capacity, BLK, HD)
    glob_kv = glob_in.transpose(1, 0, 2).reshape(GLOB, 2, BLK, kv_dev, HD).transpose(1, 0, 2, 3, 4)

    window_blocks = padded.reshape(2, block_rows + 2, BLK, kv_dev, HD)
    window_set = jnp.stack([window_blocks[:, offset : offset + block_rows] for offset in range(3)], axis=2)
    glob_set = jnp.broadcast_to(glob_kv[:, None], (2, block_rows, GLOB, BLK, kv_dev, HD))
    near_set = jnp.concatenate([window_set, glob_set], axis=2).reshape(
        2, block_rows, (3 + GLOB) * BLK, kv_dev, HD
    )
    window_ids = (
        my_index * block_rows + jnp.arange(block_rows)[:, None] + jnp.arange(-1, 2)[None, :]
    )
    window_ok = (window_ids >= 0) & (window_ids < seq_count * block_rows)
    near_ok = jnp.concatenate([window_ok, jnp.ones((block_rows, GLOB), dtype=bool)], axis=1)
    near_mask = jnp.repeat(near_ok, BLK, axis=1)

    query_nat = q_rot.reshape(block_rows, BLK, kv_dev, GROUP, HD)
    grad_nat = out_grad.reshape(block_rows, BLK, kv_dev, GROUP, HD)
    near_k = near_set[0]
    near_v = near_set[1]
    far_k = fetched_k[slot_pos].reshape(block_rows, kv_dev, RND * BLK, HD)
    far_v = fetched_v[slot_pos].reshape(block_rows, kv_dev, RND * BLK, HD)
    near_scores = (
        jnp.einsum("rthgd,rkhd->rhgtk", query_nat, near_k, preferred_element_type=jnp.float32)
        * score_scale
    )
    near_scores = jnp.where(near_mask[:, None, None, None, :], near_scores, NEG_FILL)
    far_scores = (
        jnp.einsum("rthgd,rhkd->rhgtk", query_nat, far_k, preferred_element_type=jnp.float32)
        * score_scale
    )
    row_max = jnp.maximum(
        jnp.max(near_scores, axis=-1, keepdims=True), jnp.max(far_scores, axis=-1, keepdims=True)
    )
    near_exp = jnp.exp(near_scores - row_max)
    far_exp = jnp.exp(far_scores - row_max)
    total = jnp.sum(near_exp, axis=-1, keepdims=True) + jnp.sum(far_exp, axis=-1, keepdims=True)
    near_prob = near_exp / total
    far_prob = far_exp / total
    near_w = near_prob.astype(jnp.bfloat16)
    far_w = far_prob.astype(jnp.bfloat16)

    far_vgrad = jnp.einsum("rhgtk,rthgd->rhkd", far_w, grad_nat, preferred_element_type=jnp.float32)
    out_v = jnp.einsum(
        "ps,pte->ste",
        onehot(slot_pos, seq_count * capacity),
        far_vgrad.astype(jnp.bfloat16).reshape(slot_count, BLK, HD),
        preferred_element_type=jnp.float32,
    ).astype(jnp.bfloat16)
    returned_v = exchange(out_v.reshape(seq_count, capacity * BLK, HD)).reshape(
        seq_count * capacity, BLK, HD
    )

    near_wgrad = jnp.einsum("rthgd,rkhd->rhgtk", grad_nat, near_v, preferred_element_type=jnp.float32)
    far_wgrad = jnp.einsum("rthgd,rhkd->rhgtk", grad_nat, far_v, preferred_element_type=jnp.float32)
    attended = (
        jnp.einsum("rhgtk,rkhd->rthgd", near_w, near_v, preferred_element_type=jnp.float32)
        + jnp.einsum("rhgtk,rhkd->rthgd", far_w, far_v, preferred_element_type=jnp.float32)
    ).astype(jnp.bfloat16)
    row_delta = jnp.sum(grad_nat.astype(jnp.float32) * attended.astype(jnp.float32), axis=-1)
    row_delta = row_delta.transpose(0, 2, 3, 1)[..., None]
    near_sgrad = (near_prob * (near_wgrad - row_delta) * score_scale).astype(jnp.bfloat16)
    far_sgrad = (far_prob * (far_wgrad - row_delta) * score_scale).astype(jnp.bfloat16)

    far_kgrad = jnp.einsum("rhgtk,rthgd->rhkd", far_sgrad, query_nat, preferred_element_type=jnp.float32)
    out_k = jnp.einsum(
        "ps,pte->ste",
        onehot(slot_pos, seq_count * capacity),
        far_kgrad.astype(jnp.bfloat16).reshape(slot_count, BLK, HD),
        preferred_element_type=jnp.float32,
    ).astype(jnp.bfloat16).reshape(seq_count, capacity * BLK, HD)
    near_kgrad = jnp.einsum("rhgtk,rthgd->rkhd", near_sgrad, query_nat, preferred_element_type=jnp.float32)
    near_vgrad = jnp.einsum("rhgtk,rthgd->rkhd", near_w, grad_nat, preferred_element_type=jnp.float32)
    near_grad = jnp.stack([near_kgrad, near_vgrad]).reshape(2, block_rows, 3 + GLOB, BLK, kv_dev, HD)
    glob_local_grad = jnp.sum(near_grad[:, :, 3:], axis=1)
    glob_split = glob_local_grad.transpose(1, 0, 2, 3, 4).reshape(GLOB, seq_count, piece)
    glob_split = glob_split.transpose(1, 0, 2).reshape(seq_count, glob_rows, HD)
    glob_high = glob_split.astype(jnp.bfloat16)
    glob_low = (glob_split - glob_high.astype(jnp.float32)).astype(jnp.bfloat16)
    query_portion = jnp.einsum(
        "rhgtk,rkhd->rthgd", near_sgrad, near_k, preferred_element_type=jnp.float32
    ) + jnp.einsum("rhgtk,rhkd->rthgd", far_sgrad, far_k, preferred_element_type=jnp.float32)
    query_grad = (
        unrotate(query_portion.reshape(tok_rows, kv_dev * GROUP, HD), cosines, sine_vals)
        .astype(jnp.bfloat16)
        .reshape(tok_rows, kv_dev * GROUP * HD)
    )
    payload_k = jnp.concatenate([out_k, glob_high, glob_low], axis=1)
    payload_k, query_grad = lax.optimization_barrier((payload_k, query_grad))
    returned_k = exchange(payload_k)
    glob_back = returned_k[:, capacity * BLK :].astype(jnp.float32)
    piece_sum = jnp.sum(glob_back[:, :glob_rows] + glob_back[:, glob_rows:], axis=0).reshape(GLOB, piece)
    returned_k = returned_k[:, : capacity * BLK].reshape(seq_count * capacity, BLK, HD)
    to_owner = jnp.where(
        jnp.arange(seq_count)[:, None, None] == glob_owner[None, :, None], piece_sum[None], 0.0
    )
    glob_grad = exchange(to_owner).transpose(1, 0, 2).reshape(GLOB, 2, BLK, kv_dev, HD)

    window_acc = jnp.pad(near_grad[:, :, 0], ((0, 0), (0, 2), (0, 0), (0, 0), (0, 0)))
    window_acc = window_acc + jnp.pad(near_grad[:, :, 1], ((0, 0), (1, 1), (0, 0), (0, 0), (0, 0)))
    window_acc = window_acc + jnp.pad(near_grad[:, :, 2], ((0, 0), (2, 0), (0, 0), (0, 0), (0, 0)))
    from_right = shifted(window_acc[:, 0].astype(jnp.bfloat16), "seq", -1).astype(jnp.float32)
    from_left = shifted(window_acc[:, block_rows + 1].astype(jnp.bfloat16), "seq", 1).astype(jnp.float32)

    kv_grad = window_acc[:, 1 : block_rows + 1]
    kv_grad = kv_grad.at[:, block_rows - 1].add(from_right).at[:, 0].add(from_left)
    oh_back = onehot(asked_flat, table_rows).T
    collected = jnp.stack(
        [
            jnp.einsum("qs,ste->qte", oh_back, returned_k, preferred_element_type=jnp.float32),
            jnp.einsum("qs,ste->qte", oh_back, returned_v, preferred_element_type=jnp.float32),
        ]
    ).reshape(2, block_rows, kv_dev, BLK, HD)
    kv_grad = kv_grad + collected.transpose(0, 1, 3, 2, 4)
    key_rest = unrotate(kv_grad[0].reshape(tok_rows, kv_dev, HD), cosines, sine_vals)
    key_rest = key_rest.reshape(block_rows, BLK, kv_dev, HD)
    value_rest = kv_grad[1]
    glob_mine = jnp.where((glob_owner == my_index)[:, None, None, None, None], glob_grad, 0.0)
    for which_glob in range(GLOB):
        glob_keys = unrotate(glob_mine[which_glob, 0], glob_cos[which_glob], glob_sin[which_glob])
        key_rest = key_rest.at[glob_local[which_glob]].add(glob_keys)
        value_rest = value_rest.at[glob_local[which_glob]].add(glob_mine[which_glob, 1])

    attended = attended.reshape(tok_rows, kv_dev * GROUP * HD)
    key_grad = key_rest.astype(jnp.bfloat16).reshape(tok_rows, kv_dev * HD)
    value_grad = value_rest.reshape(tok_rows, kv_dev * HD).astype(jnp.bfloat16)
    return (attended, query_grad, key_grad, value_grad)


def solution(mesh):
    in_specs = (
        P("seq", "head"),
        P("seq", "head"),
        P("seq", "head"),
        P(None, "seq"),
        P("seq", "head", None),
        P(),
        P("seq", "head"),
    )
    out_specs = (P("seq", "head"), P("seq", "head"), P("seq", "head"), P("seq", "head"))
    return jax.shard_map(local, mesh=mesh, in_specs=in_specs, out_specs=out_specs, check_vma=False)
```

```python
import math

import jax
import jax.numpy as jnp
from jax import lax
from jax.sharding import PartitionSpec as P

HD = 128
GROUP = 4
BLK = 64
GLOB = 2
RND = 3


NEG_FILL = -1e30
ROPE_BASE = 1000000.0


def extended(array, sides, width):
    for axis, dim in sides:
        devices, length = (lax.axis_size(axis), array.shape[dim])
        up = [(i, (i + 1) % devices) for i in range(devices - 1)]
        down = [(j, i) for i, j in up]
        last = lax.slice_in_dim(array, length - width, length, axis=dim)
        leading = lax.slice_in_dim(array, 0, width, axis=dim)
        before = lax.ppermute(last, axis, up)
        after = lax.ppermute(leading, axis, down)
        array = jnp.concatenate([before, array, after], axis=dim)
    return array


def spread(block, axis, source):
    block = jnp.where(lax.axis_index(axis) == source, block, jnp.zeros_like(block))
    return lax.psum(block, axis)


def shifted(array, axis, by):
    devices = lax.axis_size(axis)
    pairs = [(i, i + by) for i in range(devices) if 0 <= i + by < devices]
    return lax.ppermute(array, axis, pairs)


def tables(positions):
    half_dim = HD // 2
    freq_ids = jnp.arange(half_dim)
    inv_freq = jnp.power(jnp.float32(ROPE_BASE), -2.0 * freq_ids.astype(jnp.float32) / HD)
    pos_float = positions.astype(jnp.float32)
    chosen = jnp.where(
        (freq_ids % 3 == 0)[None, :],
        pos_float[0][:, None],
        jnp.where((freq_ids % 3 == 1)[None, :], pos_float[1][:, None], pos_float[2][:, None]),
    )
    angles = chosen * inv_freq[None, :]
    return (jnp.cos(angles), jnp.sin(angles))


def rotate(states, cosines, sine_vals):
    half_dim = HD // 2
    first_half = states[..., :half_dim]
    second_half = states[..., half_dim:]
    cos_b = cosines[:, None, :]
    sin_b = sine_vals[:, None, :]
    return jnp.concatenate(
        [first_half * cos_b - second_half * sin_b, second_half * cos_b + first_half * sin_b],
        axis=-1,
    )


def unrotate(states, cosines, sine_vals):
    half_dim = HD // 2
    first_half = states[..., :half_dim]
    second_half = states[..., half_dim:]
    cos_b = cosines[:, None, :]
    sin_b = sine_vals[:, None, :]
    return jnp.concatenate(
        [first_half * cos_b + second_half * sin_b, second_half * cos_b - first_half * sin_b],
        axis=-1,
    )


def attend(query_block_view, key_block_view, value_block_view, gradient_block_view, key_mask):
    score_scale = 1.0 / math.sqrt(HD)
    logit_scores = (
        jnp.einsum(
            "mtyp,mop->myto", query_block_view, key_block_view, preferred_element_type=jnp.float32
        )
        * score_scale
    )
    logit_scores = jnp.where(key_mask[:, None, None, :], logit_scores, NEG_FILL)
    row_max = jnp.max(logit_scores, axis=-1, keepdims=True)
    exponent = jnp.exp(logit_scores - row_max)
    probability = exponent / jnp.sum(exponent, axis=-1, keepdims=True)
    attention_weights = probability.astype(jnp.bfloat16)
    attended = jnp.einsum(
        "ywiu,yuz->yiwz", attention_weights, value_block_view, preferred_element_type=jnp.float32
    ).astype(jnp.bfloat16)
    weight_gradient = jnp.einsum(
        "mtyp,mop->myto", gradient_block_view, value_block_view, preferred_element_type=jnp.float32
    )
    row_delta = jnp.sum(
        gradient_block_view.astype(jnp.float32) * attended.astype(jnp.float32), axis=-1
    )
    row_delta = jnp.transpose(row_delta, (0, 2, 1))[..., None]
    score_gradient = (probability * (weight_gradient - row_delta) * score_scale).astype(
        jnp.bfloat16
    )
    value_portion = jnp.einsum(
        "pcht,phca->pta", attention_weights, gradient_block_view, preferred_element_type=jnp.float32
    )
    key_portion = jnp.einsum(
        "pcht,phca->pta", score_gradient, query_block_view, preferred_element_type=jnp.float32
    )
    query_portion = jnp.einsum(
        "ywiu,yuz->yiwz", score_gradient, key_block_view, preferred_element_type=jnp.float32
    )
    return (attended, query_portion, key_portion, value_portion)


def onehot(ids, count):
    return (ids[:, None] == jnp.arange(count, dtype=jnp.int32)[None, :]).astype(jnp.bfloat16)


def exchange(array):
    return lax.all_to_all(array, "seq", 0, 0, tiled=True)


def local(queries, key_states, value_states, positions, random_blocks, global_blocks, out_grad):
    tok_rows = queries.shape[0]
    block_rows = tok_rows // BLK
    kv_dev = key_states.shape[1] // HD
    seq_count = lax.axis_size("seq")
    my_index = lax.axis_index("seq")
    slot_count = block_rows * kv_dev * RND
    capacity = (slot_count + seq_count - 1) // seq_count + 1
    score_scale = 1.0 / math.sqrt(HD)
    table_rows = block_rows * kv_dev
    piece = 2 * BLK * kv_dev * HD // seq_count
    glob_rows = GLOB * piece // HD
    code_cols = 128

    cosines, sine_vals = tables(positions)
    q_rot = rotate(
        queries.reshape(tok_rows, kv_dev * GROUP, HD).astype(jnp.float32), cosines, sine_vals
    ).astype(jnp.bfloat16)
    k_rot = rotate(
        key_states.reshape(tok_rows, kv_dev, HD).astype(jnp.float32), cosines, sine_vals
    ).astype(jnp.bfloat16)
    paired = jnp.stack([k_rot.reshape(tok_rows, kv_dev * HD), value_states])
    own_blocks = paired.reshape(2, block_rows, BLK, kv_dev, HD)

    flat_ids = random_blocks.reshape(slot_count)
    owners = flat_ids // block_rows
    head_ids = jnp.broadcast_to(
        jnp.arange(kv_dev, dtype=jnp.int32)[None, :, None], (block_rows, kv_dev, RND)
    ).reshape(slot_count)
    req_code = flat_ids % block_rows * kv_dev + head_ids
    slot_ids = jnp.arange(slot_count, dtype=jnp.int32)
    earlier = (owners[:, None] == owners[None, :]) & (slot_ids[None, :] < slot_ids[:, None])
    slot_pos = owners * capacity + jnp.sum(earlier, axis=1)
    request = jnp.zeros((seq_count * capacity,), jnp.int32).at[slot_pos].set(req_code)
    request = request.reshape(seq_count, capacity)
    glob_owner = global_blocks // block_rows
    glob_local = global_blocks % block_rows
    glob_scatter = []
    glob_cos, glob_sin = [], []
    for which_glob in range(GLOB):
        start = glob_local[which_glob] * BLK
        block_cos, block_sin = tables(lax.dynamic_slice_in_dim(positions, start, BLK, 1))
        glob_cos.append(block_cos)
        glob_sin.append(block_sin)
        block_keys = lax.dynamic_slice_in_dim(key_states, start, BLK, 0)
        block_keys = rotate(
            block_keys.reshape(BLK, kv_dev, HD).astype(jnp.float32), block_cos, block_sin
        ).astype(jnp.bfloat16)
        block_values = lax.dynamic_slice_in_dim(value_states, start, BLK, 0).reshape(BLK, kv_dev, HD)
        glob_piece = jnp.stack([block_keys, block_values])
        glob_piece = jnp.where(my_index == glob_owner[which_glob], glob_piece, jnp.zeros_like(glob_piece))
        glob_scatter.append(glob_piece.reshape(seq_count, piece))
    first_out = jnp.concatenate(
        glob_scatter
        + [request.astype(jnp.bfloat16), jnp.zeros((seq_count, code_cols - capacity), jnp.bfloat16)],
        axis=1,
    )
    first_in = exchange(first_out)
    asked_part = first_in[:, GLOB * piece : GLOB * piece + capacity].astype(jnp.int32)
    my_pieces = jnp.concatenate(
        [
            lax.dynamic_index_in_dim(first_in, glob_owner[g], 0, keepdims=False)[g * piece : (g + 1) * piece]
            for g in range(GLOB)
        ]
    )
    asked_flat = asked_part.reshape(seq_count * capacity)

    k_table = own_blocks[0].transpose(0, 2, 1, 3).reshape(table_rows, BLK, HD)
    v_table = own_blocks[1].transpose(0, 2, 1, 3).reshape(table_rows, BLK, HD)
    slab_table = jnp.concatenate(
        [k_table.reshape(table_rows * BLK // glob_rows, glob_rows, HD), my_pieces.reshape(1, glob_rows, HD)]
    )
    slab_ids = (asked_part[:, :, None] * (BLK // glob_rows) + jnp.arange(BLK // glob_rows)[None, None, :])
    slab_ids = jnp.concatenate(
        [
            slab_ids.reshape(seq_count, capacity * BLK // glob_rows),
            jnp.full((seq_count, 1), table_rows * BLK // glob_rows, jnp.int32),
        ],
        axis=1,
    )
    answers_k = slab_table[slab_ids].reshape(seq_count, capacity * BLK + glob_rows, HD)
    answers_v = v_table[asked_flat].reshape(seq_count, capacity * BLK, HD)
    padded = extended(paired, (("seq", 1),), BLK)
    answers_k, padded = lax.optimization_barrier((answers_k, padded))
    fetched_k = exchange(answers_k)
    answers_v, fetched_k = lax.optimization_barrier((answers_v, fetched_k))
    fetched_v = exchange(answers_v).reshape(seq_count * capacity, BLK, HD)
    glob_in = fetched_k[:, capacity * BLK :].reshape(seq_count, GLOB, piece)
    fetched_k = fetched_k[:, : capacity * BLK].reshape(seq_count * capacity, BLK, HD)
    glob_kv = glob_in.transpose(1, 0, 2).reshape(GLOB, 2, BLK, kv_dev, HD).transpose(1, 0, 2, 3, 4)

    window_blocks = padded.reshape(2, block_rows + 2, BLK, kv_dev, HD)
    window_set = jnp.stack([window_blocks[:, offset : offset + block_rows] for offset in range(3)], axis=2)
    glob_set = jnp.broadcast_to(glob_kv[:, None], (2, block_rows, GLOB, BLK, kv_dev, HD))
    near_set = jnp.concatenate([window_set, glob_set], axis=2).reshape(
        2, block_rows, (3 + GLOB) * BLK, kv_dev, HD
    )
    window_ids = (
        my_index * block_rows + jnp.arange(block_rows)[:, None] + jnp.arange(-1, 2)[None, :]
    )
    window_ok = (window_ids >= 0) & (window_ids < seq_count * block_rows)
    near_ok = jnp.concatenate([window_ok, jnp.ones((block_rows, GLOB), dtype=bool)], axis=1)
    near_mask = jnp.repeat(near_ok, BLK, axis=1)

    query_nat = q_rot.reshape(block_rows, BLK, kv_dev, GROUP, HD)
    grad_nat = out_grad.reshape(block_rows, BLK, kv_dev, GROUP, HD)
    near_k = near_set[0]
    near_v = near_set[1]
    far_k = fetched_k[slot_pos].reshape(block_rows, kv_dev, RND * BLK, HD)
    far_v = fetched_v[slot_pos].reshape(block_rows, kv_dev, RND * BLK, HD)
    near_scores = (
        jnp.einsum("rthgd,rkhd->rhgtk", query_nat, near_k, preferred_element_type=jnp.float32)
        * score_scale
    )
    near_scores = jnp.where(near_mask[:, None, None, None, :], near_scores, NEG_FILL)
    far_scores = (
        jnp.einsum("rthgd,rhkd->rhgtk", query_nat, far_k, preferred_element_type=jnp.float32)
        * score_scale
    )
    row_max = jnp.maximum(
        jnp.max(near_scores, axis=-1, keepdims=True), jnp.max(far_scores, axis=-1, keepdims=True)
    )
    near_exp = jnp.exp(near_scores - row_max)
    far_exp = jnp.exp(far_scores - row_max)
    total = jnp.sum(near_exp, axis=-1, keepdims=True) + jnp.sum(far_exp, axis=-1, keepdims=True)
    near_prob = near_exp / total
    far_prob = far_exp / total
    near_w = near_prob.astype(jnp.bfloat16)
    far_w = far_prob.astype(jnp.bfloat16)

    far_vgrad = jnp.einsum("rhgtk,rthgd->rhkd", far_w, grad_nat, preferred_element_type=jnp.float32)
    out_v = jnp.einsum(
        "ps,pte->ste",
        onehot(slot_pos, seq_count * capacity),
        far_vgrad.astype(jnp.bfloat16).reshape(slot_count, BLK, HD),
        preferred_element_type=jnp.float32,
    ).astype(jnp.bfloat16)
    returned_v = exchange(out_v.reshape(seq_count, capacity * BLK, HD)).reshape(
        seq_count * capacity, BLK, HD
    )

    near_wgrad = jnp.einsum("rthgd,rkhd->rhgtk", grad_nat, near_v, preferred_element_type=jnp.float32)
    far_wgrad = jnp.einsum("rthgd,rhkd->rhgtk", grad_nat, far_v, preferred_element_type=jnp.float32)
    attended = (
        jnp.einsum("rhgtk,rkhd->rthgd", near_w, near_v, preferred_element_type=jnp.float32)
        + jnp.einsum("rhgtk,rhkd->rthgd", far_w, far_v, preferred_element_type=jnp.float32)
    ).astype(jnp.bfloat16)
    row_delta = jnp.sum(grad_nat.astype(jnp.float32) * attended.astype(jnp.float32), axis=-1)
    row_delta = row_delta.transpose(0, 2, 3, 1)[..., None]
    near_sgrad = (near_prob * (near_wgrad - row_delta) * score_scale).astype(jnp.bfloat16)
    far_sgrad = (far_prob * (far_wgrad - row_delta) * score_scale).astype(jnp.bfloat16)

    far_kgrad = jnp.einsum("rhgtk,rthgd->rhkd", far_sgrad, query_nat, preferred_element_type=jnp.float32)
    out_k = jnp.einsum(
        "ps,pte->ste",
        onehot(slot_pos, seq_count * capacity),
        far_kgrad.astype(jnp.bfloat16).reshape(slot_count, BLK, HD),
        preferred_element_type=jnp.float32,
    ).astype(jnp.bfloat16).reshape(seq_count, capacity * BLK, HD)
    near_kgrad = jnp.einsum("rhgtk,rthgd->rkhd", near_sgrad, query_nat, preferred_element_type=jnp.float32)
    near_vgrad = jnp.einsum("rhgtk,rthgd->rkhd", near_w, grad_nat, preferred_element_type=jnp.float32)
    near_grad = jnp.stack([near_kgrad, near_vgrad]).reshape(2, block_rows, 3 + GLOB, BLK, kv_dev, HD)
    glob_local_grad = jnp.sum(near_grad[:, :, 3:], axis=1)
    glob_split = glob_local_grad.transpose(1, 0, 2, 3, 4).reshape(GLOB, seq_count, piece)
    glob_split = glob_split.transpose(1, 0, 2).reshape(seq_count, glob_rows, HD)
    glob_high = glob_split.astype(jnp.bfloat16)
    glob_low = (glob_split - glob_high.astype(jnp.float32)).astype(jnp.bfloat16)
    query_portion = jnp.einsum(
        "rhgtk,rkhd->rthgd", near_sgrad, near_k, preferred_element_type=jnp.float32
    ) + jnp.einsum("rhgtk,rhkd->rthgd", far_sgrad, far_k, preferred_element_type=jnp.float32)
    query_grad = (
        unrotate(query_portion.reshape(tok_rows, kv_dev * GROUP, HD), cosines, sine_vals)
        .astype(jnp.bfloat16)
        .reshape(tok_rows, kv_dev * GROUP * HD)
    )
    payload_k = jnp.concatenate([out_k, glob_high, glob_low], axis=1)
    payload_k, query_grad = lax.optimization_barrier((payload_k, query_grad))
    returned_k = exchange(payload_k)
    glob_back = returned_k[:, capacity * BLK :].astype(jnp.float32)
    piece_sum = jnp.sum(glob_back[:, :glob_rows] + glob_back[:, glob_rows:], axis=0).reshape(GLOB, piece)
    returned_k = returned_k[:, : capacity * BLK].reshape(seq_count * capacity, BLK, HD)
    to_owner = jnp.where(
        jnp.arange(seq_count)[:, None, None] == glob_owner[None, :, None], piece_sum[None], 0.0
    )
    glob_grad = exchange(to_owner).transpose(1, 0, 2).reshape(GLOB, 2, BLK, kv_dev, HD)

    window_acc = jnp.pad(near_grad[:, :, 0], ((0, 0), (0, 2), (0, 0), (0, 0), (0, 0)))
    window_acc = window_acc + jnp.pad(near_grad[:, :, 1], ((0, 0), (1, 1), (0, 0), (0, 0), (0, 0)))
    window_acc = window_acc + jnp.pad(near_grad[:, :, 2], ((0, 0), (2, 0), (0, 0), (0, 0), (0, 0)))
    from_right = shifted(window_acc[:, 0].astype(jnp.bfloat16), "seq", -1).astype(jnp.float32)
    from_left = shifted(window_acc[:, block_rows + 1].astype(jnp.bfloat16), "seq", 1).astype(jnp.float32)

    kv_grad = window_acc[:, 1 : block_rows + 1]
    kv_grad = kv_grad.at[:, block_rows - 1].add(from_right).at[:, 0].add(from_left)
    oh_back = onehot(asked_flat, table_rows).T
    collected = jnp.stack(
        [
            jnp.einsum("qs,ste->qte", oh_back, returned_k, preferred_element_type=jnp.float32),
            jnp.einsum("qs,ste->qte", oh_back, returned_v, preferred_element_type=jnp.float32),
        ]
    ).reshape(2, block_rows, kv_dev, BLK, HD)
    kv_grad = kv_grad + collected.transpose(0, 1, 3, 2, 4)
    key_rest = unrotate(kv_grad[0].reshape(tok_rows, kv_dev, HD), cosines, sine_vals)
    key_rest = key_rest.reshape(block_rows, BLK, kv_dev, HD)
    value_rest = kv_grad[1]
    glob_mine = jnp.where((glob_owner == my_index)[:, None, None, None, None], glob_grad, 0.0)
    for which_glob in range(GLOB):
        glob_keys = unrotate(glob_mine[which_glob, 0], glob_cos[which_glob], glob_sin[which_glob])
        key_rest = key_rest.at[glob_local[which_glob]].add(glob_keys)
        value_rest = value_rest.at[glob_local[which_glob]].add(glob_mine[which_glob, 1])

    attended = attended.reshape(tok_rows, kv_dev * GROUP * HD)
    key_grad = key_rest.astype(jnp.bfloat16).reshape(tok_rows, kv_dev * HD)
    value_grad = value_rest.reshape(tok_rows, kv_dev * HD).astype(jnp.bfloat16)
    return (attended, query_grad, key_grad, value_grad)


def solution(mesh):
    in_specs = (
        P("seq", "head"),
        P("seq", "head"),
        P("seq", "head"),
        P(None, "seq"),
        P("seq", "head", None),
        P(),
        P("seq", "head"),
    )
    out_specs = (P("seq", "head"), P("seq", "head"), P("seq", "head"), P("seq", "head"))
    return jax.shard_map(local, mesh=mesh, in_specs=in_specs, out_specs=out_specs, check_vma=False)
```

```python
import math

import jax
import jax.numpy as jnp
from jax import lax
from jax.sharding import PartitionSpec as P

HD = 128
GROUP = 4
BLK = 64
GLOB = 2
RND = 3


NEG_FILL = -1e30
ROPE_BASE = 1000000.0


def extended(array, sides, width):
    for axis, dim in sides:
        devices, length = (lax.axis_size(axis), array.shape[dim])
        up = [(i, (i + 1) % devices) for i in range(devices - 1)]
        down = [(j, i) for i, j in up]
        last = lax.slice_in_dim(array, length - width, length, axis=dim)
        leading = lax.slice_in_dim(array, 0, width, axis=dim)
        before = lax.ppermute(last, axis, up)
        after = lax.ppermute(leading, axis, down)
        array = jnp.concatenate([before, array, after], axis=dim)
    return array


def spread(block, axis, source):
    block = jnp.where(lax.axis_index(axis) == source, block, jnp.zeros_like(block))
    return lax.psum(block, axis)


def shifted(array, axis, by):
    devices = lax.axis_size(axis)
    pairs = [(i, i + by) for i in range(devices) if 0 <= i + by < devices]
    return lax.ppermute(array, axis, pairs)


def tables(positions):
    half_dim = HD // 2
    freq_ids = jnp.arange(half_dim)
    inv_freq = jnp.power(jnp.float32(ROPE_BASE), -2.0 * freq_ids.astype(jnp.float32) / HD)
    pos_float = positions.astype(jnp.float32)
    chosen = jnp.where(
        (freq_ids % 3 == 0)[None, :],
        pos_float[0][:, None],
        jnp.where((freq_ids % 3 == 1)[None, :], pos_float[1][:, None], pos_float[2][:, None]),
    )
    angles = chosen * inv_freq[None, :]
    return (jnp.cos(angles), jnp.sin(angles))


def rotate(states, cosines, sine_vals):
    half_dim = HD // 2
    first_half = states[..., :half_dim]
    second_half = states[..., half_dim:]
    cos_b = cosines[:, None, :]
    sin_b = sine_vals[:, None, :]
    return jnp.concatenate(
        [first_half * cos_b - second_half * sin_b, second_half * cos_b + first_half * sin_b],
        axis=-1,
    )


def unrotate(states, cosines, sine_vals):
    half_dim = HD // 2
    first_half = states[..., :half_dim]
    second_half = states[..., half_dim:]
    cos_b = cosines[:, None, :]
    sin_b = sine_vals[:, None, :]
    return jnp.concatenate(
        [first_half * cos_b + second_half * sin_b, second_half * cos_b - first_half * sin_b],
        axis=-1,
    )


def attend(query_block_view, key_block_view, value_block_view, gradient_block_view, key_mask):
    score_scale = 1.0 / math.sqrt(HD)
    logit_scores = (
        jnp.einsum(
            "mtyp,mop->myto", query_block_view, key_block_view, preferred_element_type=jnp.float32
        )
        * score_scale
    )
    logit_scores = jnp.where(key_mask[:, None, None, :], logit_scores, NEG_FILL)
    row_max = jnp.max(logit_scores, axis=-1, keepdims=True)
    exponent = jnp.exp(logit_scores - row_max)
    probability = exponent / jnp.sum(exponent, axis=-1, keepdims=True)
    attention_weights = probability.astype(jnp.bfloat16)
    attended = jnp.einsum(
        "ywiu,yuz->yiwz", attention_weights, value_block_view, preferred_element_type=jnp.float32
    ).astype(jnp.bfloat16)
    weight_gradient = jnp.einsum(
        "mtyp,mop->myto", gradient_block_view, value_block_view, preferred_element_type=jnp.float32
    )
    row_delta = jnp.sum(
        gradient_block_view.astype(jnp.float32) * attended.astype(jnp.float32), axis=-1
    )
    row_delta = jnp.transpose(row_delta, (0, 2, 1))[..., None]
    score_gradient = (probability * (weight_gradient - row_delta) * score_scale).astype(
        jnp.bfloat16
    )
    value_portion = jnp.einsum(
        "pcht,phca->pta", attention_weights, gradient_block_view, preferred_element_type=jnp.float32
    )
    key_portion = jnp.einsum(
        "pcht,phca->pta", score_gradient, query_block_view, preferred_element_type=jnp.float32
    )
    query_portion = jnp.einsum(
        "ywiu,yuz->yiwz", score_gradient, key_block_view, preferred_element_type=jnp.float32
    )
    return (attended, query_portion, key_portion, value_portion)


def onehot(ids, count):
    return (ids[:, None] == jnp.arange(count, dtype=jnp.int32)[None, :]).astype(jnp.bfloat16)


def exchange(array):
    return lax.all_to_all(array, "seq", 0, 0, tiled=True)


def local(queries, key_states, value_states, positions, random_blocks, global_blocks, out_grad):
    tok_rows = queries.shape[0]
    block_rows = tok_rows // BLK
    kv_dev = key_states.shape[1] // HD
    seq_count = lax.axis_size("seq")
    my_index = lax.axis_index("seq")
    slot_count = block_rows * kv_dev * RND
    capacity = (slot_count + seq_count - 1) // seq_count + 1
    score_scale = 1.0 / math.sqrt(HD)
    table_rows = block_rows * kv_dev
    piece = 2 * BLK * kv_dev * HD // seq_count
    glob_rows = GLOB * piece // HD
    code_cols = 128

    cosines, sine_vals = tables(positions)
    q_rot = rotate(
        queries.reshape(tok_rows, kv_dev * GROUP, HD).astype(jnp.float32), cosines, sine_vals
    ).astype(jnp.bfloat16)
    k_rot = rotate(
        key_states.reshape(tok_rows, kv_dev, HD).astype(jnp.float32), cosines, sine_vals
    ).astype(jnp.bfloat16)
    paired = jnp.stack([k_rot.reshape(tok_rows, kv_dev * HD), value_states])
    own_blocks = paired.reshape(2, block_rows, BLK, kv_dev, HD)

    flat_ids = random_blocks.reshape(slot_count)
    owners = flat_ids // block_rows
    head_ids = jnp.broadcast_to(
        jnp.arange(kv_dev, dtype=jnp.int32)[None, :, None], (block_rows, kv_dev, RND)
    ).reshape(slot_count)
    req_code = flat_ids % block_rows * kv_dev + head_ids
    slot_ids = jnp.arange(slot_count, dtype=jnp.int32)
    earlier = (owners[:, None] == owners[None, :]) & (slot_ids[None, :] < slot_ids[:, None])
    slot_pos = owners * capacity + jnp.sum(earlier, axis=1)
    request = jnp.zeros((seq_count * capacity,), jnp.int32).at[slot_pos].set(req_code)
    request = request.reshape(seq_count, capacity)
    glob_owner = global_blocks // block_rows
    glob_local = global_blocks % block_rows
    glob_scatter = []
    glob_cos, glob_sin = [], []
    for which_glob in range(GLOB):
        start = glob_local[which_glob] * BLK
        block_cos, block_sin = tables(lax.dynamic_slice_in_dim(positions, start, BLK, 1))
        glob_cos.append(block_cos)
        glob_sin.append(block_sin)
        block_keys = lax.dynamic_slice_in_dim(key_states, start, BLK, 0)
        block_keys = rotate(
            block_keys.reshape(BLK, kv_dev, HD).astype(jnp.float32), block_cos, block_sin
        ).astype(jnp.bfloat16)
        block_values = lax.dynamic_slice_in_dim(value_states, start, BLK, 0).reshape(BLK, kv_dev, HD)
        glob_piece = jnp.stack([block_keys, block_values])
        glob_piece = jnp.where(my_index == glob_owner[which_glob], glob_piece, jnp.zeros_like(glob_piece))
        glob_scatter.append(glob_piece.reshape(seq_count, piece))
    first_out = jnp.concatenate(
        glob_scatter
        + [request.astype(jnp.bfloat16), jnp.zeros((seq_count, code_cols - capacity), jnp.bfloat16)],
        axis=1,
    )
    first_in = exchange(first_out)
    asked_part = first_in[:, GLOB * piece : GLOB * piece + capacity].astype(jnp.int32)
    my_pieces = jnp.concatenate(
        [
            lax.dynamic_index_in_dim(first_in, glob_owner[g], 0, keepdims=False)[g * piece : (g + 1) * piece]
            for g in range(GLOB)
        ]
    )
    asked_flat = asked_part.reshape(seq_count * capacity)

    k_table = own_blocks[0].transpose(0, 2, 1, 3).reshape(table_rows, BLK, HD)
    v_table = own_blocks[1].transpose(0, 2, 1, 3).reshape(table_rows, BLK, HD)
    slab_table = jnp.concatenate(
        [k_table.reshape(table_rows * BLK // glob_rows, glob_rows, HD), my_pieces.reshape(1, glob_rows, HD)]
    )
    slab_ids = (asked_part[:, :, None] * (BLK // glob_rows) + jnp.arange(BLK // glob_rows)[None, None, :])
    slab_ids = jnp.concatenate(
        [
            slab_ids.reshape(seq_count, capacity * BLK // glob_rows),
            jnp.full((seq_count, 1), table_rows * BLK // glob_rows, jnp.int32),
        ],
        axis=1,
    )
    answers_k = slab_table[slab_ids].reshape(seq_count, capacity * BLK + glob_rows, HD)
    answers_v = v_table[asked_flat].reshape(seq_count, capacity * BLK, HD)
    padded = extended(paired, (("seq", 1),), BLK)
    answers_k, padded = lax.optimization_barrier((answers_k, padded))
    fetched_k = exchange(answers_k)
    answers_v, fetched_k = lax.optimization_barrier((answers_v, fetched_k))
    fetched_v = exchange(answers_v).reshape(seq_count * capacity, BLK, HD)
    glob_in = fetched_k[:, capacity * BLK :].reshape(seq_count, GLOB, piece)
    fetched_k = fetched_k[:, : capacity * BLK].reshape(seq_count * capacity, BLK, HD)
    glob_kv = glob_in.transpose(1, 0, 2).reshape(GLOB, 2, BLK, kv_dev, HD).transpose(1, 0, 2, 3, 4)

    window_blocks = padded.reshape(2, block_rows + 2, BLK, kv_dev, HD)
    window_set = jnp.stack([window_blocks[:, offset : offset + block_rows] for offset in range(3)], axis=2)
    glob_set = jnp.broadcast_to(glob_kv[:, None], (2, block_rows, GLOB, BLK, kv_dev, HD))
    near_set = jnp.concatenate([window_set, glob_set], axis=2).reshape(
        2, block_rows, (3 + GLOB) * BLK, kv_dev, HD
    )
    window_ids = (
        my_index * block_rows + jnp.arange(block_rows)[:, None] + jnp.arange(-1, 2)[None, :]
    )
    window_ok = (window_ids >= 0) & (window_ids < seq_count * block_rows)
    near_ok = jnp.concatenate([window_ok, jnp.ones((block_rows, GLOB), dtype=bool)], axis=1)
    near_mask = jnp.repeat(near_ok, BLK, axis=1)

    query_nat = q_rot.reshape(block_rows, BLK, kv_dev, GROUP, HD)
    grad_nat = out_grad.reshape(block_rows, BLK, kv_dev, GROUP, HD)
    near_k = near_set[0]
    near_v = near_set[1]
    far_k = fetched_k[slot_pos].reshape(block_rows, kv_dev, RND * BLK, HD)
    far_v = fetched_v[slot_pos].reshape(block_rows, kv_dev, RND * BLK, HD)
    near_scores = (
        jnp.einsum("rthgd,rkhd->rhgtk", query_nat, near_k, preferred_element_type=jnp.float32)
        * score_scale
    )
    near_scores = jnp.where(near_mask[:, None, None, None, :], near_scores, NEG_FILL)
    far_scores = (
        jnp.einsum("rthgd,rhkd->rhgtk", query_nat, far_k, preferred_element_type=jnp.float32)
        * score_scale
    )
    row_max = jnp.maximum(
        jnp.max(near_scores, axis=-1, keepdims=True), jnp.max(far_scores, axis=-1, keepdims=True)
    )
    near_exp = jnp.exp(near_scores - row_max)
    far_exp = jnp.exp(far_scores - row_max)
    total = jnp.sum(near_exp, axis=-1, keepdims=True) + jnp.sum(far_exp, axis=-1, keepdims=True)
    near_prob = near_exp / total
    far_prob = far_exp / total
    near_w = near_prob.astype(jnp.bfloat16)
    far_w = far_prob.astype(jnp.bfloat16)

    far_vgrad = jnp.einsum("rhgtk,rthgd->rhkd", far_w, grad_nat, preferred_element_type=jnp.float32)
    out_v = jnp.einsum(
        "ps,pte->ste",
        onehot(slot_pos, seq_count * capacity),
        far_vgrad.astype(jnp.bfloat16).reshape(slot_count, BLK, HD),
        preferred_element_type=jnp.float32,
    ).astype(jnp.bfloat16)
    returned_v = exchange(out_v.reshape(seq_count, capacity * BLK, HD)).reshape(
        seq_count * capacity, BLK, HD
    )

    near_wgrad = jnp.einsum("rthgd,rkhd->rhgtk", grad_nat, near_v, preferred_element_type=jnp.float32)
    far_wgrad = jnp.einsum("rthgd,rhkd->rhgtk", grad_nat, far_v, preferred_element_type=jnp.float32)
    attended = (
        jnp.einsum("rhgtk,rkhd->rthgd", near_w, near_v, preferred_element_type=jnp.float32)
        + jnp.einsum("rhgtk,rhkd->rthgd", far_w, far_v, preferred_element_type=jnp.float32)
    ).astype(jnp.bfloat16)
    row_delta = jnp.sum(grad_nat.astype(jnp.float32) * attended.astype(jnp.float32), axis=-1)
    row_delta = row_delta.transpose(0, 2, 3, 1)[..., None]
    near_sgrad = (near_prob * (near_wgrad - row_delta) * score_scale).astype(jnp.bfloat16)
    far_sgrad = (far_prob * (far_wgrad - row_delta) * score_scale).astype(jnp.bfloat16)

    far_kgrad = jnp.einsum("rhgtk,rthgd->rhkd", far_sgrad, query_nat, preferred_element_type=jnp.float32)
    out_k = jnp.einsum(
        "ps,pte->ste",
        onehot(slot_pos, seq_count * capacity),
        far_kgrad.astype(jnp.bfloat16).reshape(slot_count, BLK, HD),
        preferred_element_type=jnp.float32,
    ).astype(jnp.bfloat16).reshape(seq_count, capacity * BLK, HD)
    near_kgrad = jnp.einsum("rhgtk,rthgd->rkhd", near_sgrad, query_nat, preferred_element_type=jnp.float32)
    near_vgrad = jnp.einsum("rhgtk,rthgd->rkhd", near_w, grad_nat, preferred_element_type=jnp.float32)
    near_grad = jnp.stack([near_kgrad, near_vgrad]).reshape(2, block_rows, 3 + GLOB, BLK, kv_dev, HD)
    glob_local_grad = jnp.sum(near_grad[:, :, 3:], axis=1)
    glob_split = glob_local_grad.transpose(1, 0, 2, 3, 4).reshape(GLOB, seq_count, piece)
    glob_split = glob_split.transpose(1, 0, 2).reshape(seq_count, glob_rows, HD)
    glob_high = glob_split.astype(jnp.bfloat16)
    glob_low = (glob_split - glob_high.astype(jnp.float32)).astype(jnp.bfloat16)
    query_portion = jnp.einsum(
        "rhgtk,rkhd->rthgd", near_sgrad, near_k, preferred_element_type=jnp.float32
    ) + jnp.einsum("rhgtk,rhkd->rthgd", far_sgrad, far_k, preferred_element_type=jnp.float32)
    query_grad = (
        unrotate(query_portion.reshape(tok_rows, kv_dev * GROUP, HD), cosines, sine_vals)
        .astype(jnp.bfloat16)
        .reshape(tok_rows, kv_dev * GROUP * HD)
    )
    payload_k = jnp.concatenate([out_k, glob_high, glob_low], axis=1)
    payload_k, query_grad = lax.optimization_barrier((payload_k, query_grad))
    returned_k = exchange(payload_k)
    glob_back = returned_k[:, capacity * BLK :].astype(jnp.float32)
    piece_sum = jnp.sum(glob_back[:, :glob_rows] + glob_back[:, glob_rows:], axis=0).reshape(GLOB, piece)
    returned_k = returned_k[:, : capacity * BLK].reshape(seq_count * capacity, BLK, HD)
    to_owner = jnp.where(
        jnp.arange(seq_count)[:, None, None] == glob_owner[None, :, None], piece_sum[None], 0.0
    )
    to_owner = to_owner.reshape(seq_count, glob_rows, HD)
    glob_grad = exchange(to_owner).reshape(seq_count, GLOB, piece)
    glob_grad = glob_grad.transpose(1, 0, 2).reshape(GLOB, 2, BLK, kv_dev, HD)

    window_acc = jnp.pad(near_grad[:, :, 0], ((0, 0), (0, 2), (0, 0), (0, 0), (0, 0)))
    window_acc = window_acc + jnp.pad(near_grad[:, :, 1], ((0, 0), (1, 1), (0, 0), (0, 0), (0, 0)))
    window_acc = window_acc + jnp.pad(near_grad[:, :, 2], ((0, 0), (2, 0), (0, 0), (0, 0), (0, 0)))
    from_right = shifted(window_acc[:, 0].astype(jnp.bfloat16), "seq", -1).astype(jnp.float32)
    from_left = shifted(window_acc[:, block_rows + 1].astype(jnp.bfloat16), "seq", 1).astype(jnp.float32)

    kv_grad = window_acc[:, 1 : block_rows + 1]
    kv_grad = kv_grad.at[:, block_rows - 1].add(from_right).at[:, 0].add(from_left)
    oh_back = onehot(asked_flat, table_rows).T
    collected = jnp.stack(
        [
            jnp.einsum("qs,ste->qte", oh_back, returned_k, preferred_element_type=jnp.float32),
            jnp.einsum("qs,ste->qte", oh_back, returned_v, preferred_element_type=jnp.float32),
        ]
    ).reshape(2, block_rows, kv_dev, BLK, HD)
    kv_grad = kv_grad + collected.transpose(0, 1, 3, 2, 4)
    key_rest = unrotate(kv_grad[0].reshape(tok_rows, kv_dev, HD), cosines, sine_vals)
    key_rest = key_rest.reshape(block_rows, BLK, kv_dev, HD)
    value_rest = kv_grad[1]
    glob_mine = jnp.where((glob_owner == my_index)[:, None, None, None, None], glob_grad, 0.0)
    for which_glob in range(GLOB):
        glob_keys = unrotate(glob_mine[which_glob, 0], glob_cos[which_glob], glob_sin[which_glob])
        key_rest = key_rest.at[glob_local[which_glob]].add(glob_keys)
        value_rest = value_rest.at[glob_local[which_glob]].add(glob_mine[which_glob, 1])

    attended = attended.reshape(tok_rows, kv_dev * GROUP * HD)
    key_grad = key_rest.astype(jnp.bfloat16).reshape(tok_rows, kv_dev * HD)
    value_grad = value_rest.reshape(tok_rows, kv_dev * HD).astype(jnp.bfloat16)
    return (attended, query_grad, key_grad, value_grad)


def solution(mesh):
    in_specs = (
        P("seq", "head"),
        P("seq", "head"),
        P("seq", "head"),
        P(None, "seq"),
        P("seq", "head", None),
        P(),
        P("seq", "head"),
    )
    out_specs = (P("seq", "head"), P("seq", "head"), P("seq", "head"), P("seq", "head"))
    return jax.shard_map(local, mesh=mesh, in_specs=in_specs, out_specs=out_specs, check_vma=False)
```

```python
import math

import jax
import jax.numpy as jnp
from jax import lax
from jax.sharding import PartitionSpec as P

HD = 128
GROUP = 4
BLK = 64
GLOB = 2
RND = 3


NEG_FILL = -1e30
ROPE_BASE = 1000000.0


def extended(array, sides, width):
    for axis, dim in sides:
        devices, length = (lax.axis_size(axis), array.shape[dim])
        up = [(i, (i + 1) % devices) for i in range(devices - 1)]
        down = [(j, i) for i, j in up]
        last = lax.slice_in_dim(array, length - width, length, axis=dim)
        leading = lax.slice_in_dim(array, 0, width, axis=dim)
        before = lax.ppermute(last, axis, up)
        after = lax.ppermute(leading, axis, down)
        array = jnp.concatenate([before, array, after], axis=dim)
    return array


def spread(block, axis, source):
    block = jnp.where(lax.axis_index(axis) == source, block, jnp.zeros_like(block))
    return lax.psum(block, axis)


def shifted(array, axis, by):
    devices = lax.axis_size(axis)
    pairs = [(i, i + by) for i in range(devices) if 0 <= i + by < devices]
    return lax.ppermute(array, axis, pairs)


def tables(positions):
    half_dim = HD // 2
    freq_ids = jnp.arange(half_dim)
    inv_freq = jnp.power(jnp.float32(ROPE_BASE), -2.0 * freq_ids.astype(jnp.float32) / HD)
    pos_float = positions.astype(jnp.float32)
    chosen = jnp.where(
        (freq_ids % 3 == 0)[None, :],
        pos_float[0][:, None],
        jnp.where((freq_ids % 3 == 1)[None, :], pos_float[1][:, None], pos_float[2][:, None]),
    )
    angles = chosen * inv_freq[None, :]
    return (jnp.cos(angles), jnp.sin(angles))


def rotate(states, cosines, sine_vals):
    half_dim = HD // 2
    first_half = states[..., :half_dim]
    second_half = states[..., half_dim:]
    cos_b = cosines[:, None, :]
    sin_b = sine_vals[:, None, :]
    return jnp.concatenate(
        [first_half * cos_b - second_half * sin_b, second_half * cos_b + first_half * sin_b],
        axis=-1,
    )


def unrotate(states, cosines, sine_vals):
    half_dim = HD // 2
    first_half = states[..., :half_dim]
    second_half = states[..., half_dim:]
    cos_b = cosines[:, None, :]
    sin_b = sine_vals[:, None, :]
    return jnp.concatenate(
        [first_half * cos_b + second_half * sin_b, second_half * cos_b - first_half * sin_b],
        axis=-1,
    )


def attend(query_block_view, key_block_view, value_block_view, gradient_block_view, key_mask):
    score_scale = 1.0 / math.sqrt(HD)
    logit_scores = (
        jnp.einsum(
            "mtyp,mop->myto", query_block_view, key_block_view, preferred_element_type=jnp.float32
        )
        * score_scale
    )
    logit_scores = jnp.where(key_mask[:, None, None, :], logit_scores, NEG_FILL)
    row_max = jnp.max(logit_scores, axis=-1, keepdims=True)
    exponent = jnp.exp(logit_scores - row_max)
    probability = exponent / jnp.sum(exponent, axis=-1, keepdims=True)
    attention_weights = probability.astype(jnp.bfloat16)
    attended = jnp.einsum(
        "ywiu,yuz->yiwz", attention_weights, value_block_view, preferred_element_type=jnp.float32
    ).astype(jnp.bfloat16)
    weight_gradient = jnp.einsum(
        "mtyp,mop->myto", gradient_block_view, value_block_view, preferred_element_type=jnp.float32
    )
    row_delta = jnp.sum(
        gradient_block_view.astype(jnp.float32) * attended.astype(jnp.float32), axis=-1
    )
    row_delta = jnp.transpose(row_delta, (0, 2, 1))[..., None]
    score_gradient = (probability * (weight_gradient - row_delta) * score_scale).astype(
        jnp.bfloat16
    )
    value_portion = jnp.einsum(
        "pcht,phca->pta", attention_weights, gradient_block_view, preferred_element_type=jnp.float32
    )
    key_portion = jnp.einsum(
        "pcht,phca->pta", score_gradient, query_block_view, preferred_element_type=jnp.float32
    )
    query_portion = jnp.einsum(
        "ywiu,yuz->yiwz", score_gradient, key_block_view, preferred_element_type=jnp.float32
    )
    return (attended, query_portion, key_portion, value_portion)


def onehot(ids, count):
    return (ids[:, None] == jnp.arange(count, dtype=jnp.int32)[None, :]).astype(jnp.bfloat16)


def exchange(array):
    return lax.all_to_all(array, "seq", 0, 0, tiled=True)


def pick(ids, table):
    return jnp.einsum(
        "sq,qte->ste", onehot(ids, table.shape[0]), table, preferred_element_type=jnp.float32
    )


def local(queries, key_states, value_states, positions, random_blocks, global_blocks, out_grad):
    tok_rows = queries.shape[0]
    block_rows = tok_rows // BLK
    kv_dev = key_states.shape[1] // HD
    seq_count = lax.axis_size("seq")
    my_index = lax.axis_index("seq")
    slot_count = block_rows * kv_dev * RND
    capacity = (slot_count + seq_count - 1) // seq_count + 1
    score_scale = 1.0 / math.sqrt(HD)
    table_rows = block_rows * kv_dev
    piece = 2 * BLK * kv_dev * HD // seq_count
    glob_rows = GLOB * piece // HD
    code_cols = 128

    cosines, sine_vals = tables(positions)
    q_rot = rotate(
        queries.reshape(tok_rows, kv_dev * GROUP, HD).astype(jnp.float32), cosines, sine_vals
    ).astype(jnp.bfloat16)
    k_rot = rotate(
        key_states.reshape(tok_rows, kv_dev, HD).astype(jnp.float32), cosines, sine_vals
    ).astype(jnp.bfloat16)
    paired = jnp.stack([k_rot.reshape(tok_rows, kv_dev * HD), value_states])
    own_blocks = paired.reshape(2, block_rows, BLK, kv_dev, HD)

    flat_ids = random_blocks.reshape(slot_count)
    owners = flat_ids // block_rows
    head_ids = jnp.broadcast_to(
        jnp.arange(kv_dev, dtype=jnp.int32)[None, :, None], (block_rows, kv_dev, RND)
    ).reshape(slot_count)
    req_code = flat_ids % block_rows * kv_dev + head_ids
    slot_ids = jnp.arange(slot_count, dtype=jnp.int32)
    earlier = (owners[:, None] == owners[None, :]) & (slot_ids[None, :] < slot_ids[:, None])
    slot_pos = owners * capacity + jnp.sum(earlier, axis=1)
    request = jnp.sum(
        jnp.where(
            slot_pos[None, :] == jnp.arange(seq_count * capacity, dtype=jnp.int32)[:, None],
            req_code[None, :],
            0,
        ),
        axis=1,
    ).reshape(seq_count, capacity)
    glob_owner = global_blocks // block_rows
    glob_local = global_blocks % block_rows
    glob_tokens = (glob_local[:, None] * BLK + jnp.arange(BLK, dtype=jnp.int32)[None, :]).reshape(GLOB * BLK)
    both_cos, both_sin = tables(positions[:, glob_tokens])
    glob_cos = [both_cos[g * BLK : (g + 1) * BLK] for g in range(GLOB)]
    glob_sin = [both_sin[g * BLK : (g + 1) * BLK] for g in range(GLOB)]
    glob_keys = rotate(
        key_states[glob_tokens].reshape(GLOB * BLK, kv_dev, HD).astype(jnp.float32), both_cos, both_sin
    ).astype(jnp.bfloat16)
    glob_values = value_states[glob_tokens].reshape(GLOB * BLK, kv_dev, HD)
    glob_both = jnp.stack([glob_keys, glob_values]).reshape(2, GLOB, BLK, kv_dev, HD)
    glob_both = jnp.where(
        (my_index == glob_owner)[None, :, None, None, None], glob_both, jnp.zeros_like(glob_both)
    )
    glob_scatter = [
        glob_both.transpose(1, 0, 2, 3, 4).reshape(GLOB, seq_count, piece).transpose(1, 0, 2).reshape(
            seq_count, GLOB * piece
        )
    ]
    first_out = jnp.concatenate(
        glob_scatter
        + [request.astype(jnp.bfloat16), jnp.zeros((seq_count, code_cols - capacity), jnp.bfloat16)],
        axis=1,
    )
    first_in = exchange(first_out)
    asked_part = first_in[:, GLOB * piece : GLOB * piece + capacity].astype(jnp.int32)
    my_pieces = jnp.concatenate(
        [
            lax.dynamic_index_in_dim(first_in, glob_owner[g], 0, keepdims=False)[g * piece : (g + 1) * piece]
            for g in range(GLOB)
        ]
    )
    asked_flat = asked_part.reshape(seq_count * capacity)

    k_table = own_blocks[0].transpose(0, 2, 1, 3).reshape(table_rows, BLK, HD)
    v_table = own_blocks[1].transpose(0, 2, 1, 3).reshape(table_rows, BLK, HD)
    answers_k = pick(asked_flat, k_table).astype(jnp.bfloat16).reshape(seq_count, capacity * BLK, HD)
    answers_k = jnp.concatenate(
        [answers_k, jnp.broadcast_to(my_pieces.reshape(1, glob_rows, HD), (seq_count, glob_rows, HD))],
        axis=1,
    )
    answers_v = pick(asked_flat, v_table).astype(jnp.bfloat16).reshape(seq_count, capacity * BLK, HD)
    padded = extended(paired, (("seq", 1),), BLK)
    answers_k, padded = lax.optimization_barrier((answers_k, padded))
    fetched_k = exchange(answers_k)
    answers_v, fetched_k = lax.optimization_barrier((answers_v, fetched_k))
    fetched_v = exchange(answers_v).reshape(seq_count * capacity, BLK, HD)
    glob_in = fetched_k[:, capacity * BLK :].reshape(seq_count, GLOB, piece)
    fetched_k = fetched_k[:, : capacity * BLK].reshape(seq_count * capacity, BLK, HD)
    glob_kv = glob_in.transpose(1, 0, 2).reshape(GLOB, 2, BLK, kv_dev, HD).transpose(1, 0, 2, 3, 4)

    window_blocks = padded.reshape(2, block_rows + 2, BLK, kv_dev, HD)
    window_set = jnp.stack([window_blocks[:, offset : offset + block_rows] for offset in range(3)], axis=2)
    glob_set = jnp.broadcast_to(glob_kv[:, None], (2, block_rows, GLOB, BLK, kv_dev, HD))
    near_set = jnp.concatenate([window_set, glob_set], axis=2).reshape(
        2, block_rows, (3 + GLOB) * BLK, kv_dev, HD
    )
    window_ids = (
        my_index * block_rows + jnp.arange(block_rows)[:, None] + jnp.arange(-1, 2)[None, :]
    )
    window_ok = (window_ids >= 0) & (window_ids < seq_count * block_rows)
    near_ok = jnp.concatenate([window_ok, jnp.ones((block_rows, GLOB), dtype=bool)], axis=1)
    near_mask = jnp.repeat(near_ok, BLK, axis=1)

    query_nat = q_rot.reshape(block_rows, BLK, kv_dev, GROUP, HD)
    grad_nat = out_grad.reshape(block_rows, BLK, kv_dev, GROUP, HD)
    near_k = near_set[0]
    near_v = near_set[1]
    far_k = fetched_k[slot_pos].reshape(block_rows, kv_dev, RND * BLK, HD)
    far_v = fetched_v[slot_pos].reshape(block_rows, kv_dev, RND * BLK, HD)
    near_scores = (
        jnp.einsum("rthgd,rkhd->rhgtk", query_nat, near_k, preferred_element_type=jnp.float32)
        * score_scale
    )
    near_scores = jnp.where(near_mask[:, None, None, None, :], near_scores, NEG_FILL)
    far_scores = (
        jnp.einsum("rthgd,rhkd->rhgtk", query_nat, far_k, preferred_element_type=jnp.float32)
        * score_scale
    )
    row_max = jnp.maximum(
        jnp.max(near_scores, axis=-1, keepdims=True), jnp.max(far_scores, axis=-1, keepdims=True)
    )
    near_exp = jnp.exp(near_scores - row_max)
    far_exp = jnp.exp(far_scores - row_max)
    total = jnp.sum(near_exp, axis=-1, keepdims=True) + jnp.sum(far_exp, axis=-1, keepdims=True)
    near_prob = near_exp / total
    far_prob = far_exp / total
    near_w = near_prob.astype(jnp.bfloat16)
    far_w = far_prob.astype(jnp.bfloat16)

    far_vgrad = jnp.einsum("rhgtk,rthgd->rhkd", far_w, grad_nat, preferred_element_type=jnp.float32)
    out_v = jnp.einsum(
        "ps,pte->ste",
        onehot(slot_pos, seq_count * capacity),
        far_vgrad.astype(jnp.bfloat16).reshape(slot_count, BLK, HD),
        preferred_element_type=jnp.float32,
    ).astype(jnp.bfloat16)
    returned_v = exchange(out_v.reshape(seq_count, capacity * BLK, HD)).reshape(
        seq_count * capacity, BLK, HD
    )

    near_wgrad = jnp.einsum("rthgd,rkhd->rhgtk", grad_nat, near_v, preferred_element_type=jnp.float32)
    far_wgrad = jnp.einsum("rthgd,rhkd->rhgtk", grad_nat, far_v, preferred_element_type=jnp.float32)
    attended = (
        jnp.einsum("rhgtk,rkhd->rthgd", near_w, near_v, preferred_element_type=jnp.float32)
        + jnp.einsum("rhgtk,rhkd->rthgd", far_w, far_v, preferred_element_type=jnp.float32)
    ).astype(jnp.bfloat16)
    row_delta = jnp.sum(grad_nat.astype(jnp.float32) * attended.astype(jnp.float32), axis=-1)
    row_delta = row_delta.transpose(0, 2, 3, 1)[..., None]
    near_sgrad = (near_prob * (near_wgrad - row_delta) * score_scale).astype(jnp.bfloat16)
    far_sgrad = (far_prob * (far_wgrad - row_delta) * score_scale).astype(jnp.bfloat16)

    far_kgrad = jnp.einsum("rhgtk,rthgd->rhkd", far_sgrad, query_nat, preferred_element_type=jnp.float32)
    out_k = jnp.einsum(
        "ps,pte->ste",
        onehot(slot_pos, seq_count * capacity),
        far_kgrad.astype(jnp.bfloat16).reshape(slot_count, BLK, HD),
        preferred_element_type=jnp.float32,
    ).astype(jnp.bfloat16).reshape(seq_count, capacity * BLK, HD)
    near_kgrad = jnp.einsum("rhgtk,rthgd->rkhd", near_sgrad, query_nat, preferred_element_type=jnp.float32)
    near_vgrad = jnp.einsum("rhgtk,rthgd->rkhd", near_w, grad_nat, preferred_element_type=jnp.float32)
    near_grad = jnp.stack([near_kgrad, near_vgrad]).reshape(2, block_rows, 3 + GLOB, BLK, kv_dev, HD)
    glob_local_grad = jnp.sum(near_grad[:, :, 3:], axis=1)
    glob_split = glob_local_grad.transpose(1, 0, 2, 3, 4).reshape(GLOB, seq_count, piece)
    glob_split = glob_split.transpose(1, 0, 2).reshape(seq_count, glob_rows, HD)
    glob_high = glob_split.astype(jnp.bfloat16)
    glob_low = (glob_split - glob_high.astype(jnp.float32)).astype(jnp.bfloat16)
    query_portion = jnp.einsum(
        "rhgtk,rkhd->rthgd", near_sgrad, near_k, preferred_element_type=jnp.float32
    ) + jnp.einsum("rhgtk,rhkd->rthgd", far_sgrad, far_k, preferred_element_type=jnp.float32)
    query_grad = (
        unrotate(query_portion.reshape(tok_rows, kv_dev * GROUP, HD), cosines, sine_vals)
        .astype(jnp.bfloat16)
        .reshape(tok_rows, kv_dev * GROUP * HD)
    )
    payload_k = jnp.concatenate([out_k, glob_high, glob_low], axis=1)
    payload_k, query_grad = lax.optimization_barrier((payload_k, query_grad))
    returned_k = exchange(payload_k)
    glob_back = returned_k[:, capacity * BLK :].astype(jnp.float32)
    piece_sum = jnp.sum(glob_back[:, :glob_rows] + glob_back[:, glob_rows:], axis=0).reshape(GLOB, piece)
    returned_k = returned_k[:, : capacity * BLK].reshape(seq_count * capacity, BLK, HD)
    to_owner = jnp.where(
        jnp.arange(seq_count)[:, None, None] == glob_owner[None, :, None], piece_sum[None], 0.0
    )
    glob_grad = exchange(to_owner).transpose(1, 0, 2).reshape(GLOB, 2, BLK, kv_dev, HD)

    window_acc = jnp.pad(near_grad[:, :, 0], ((0, 0), (0, 2), (0, 0), (0, 0), (0, 0)))
    window_acc = window_acc + jnp.pad(near_grad[:, :, 1], ((0, 0), (1, 1), (0, 0), (0, 0), (0, 0)))
    window_acc = window_acc + jnp.pad(near_grad[:, :, 2], ((0, 0), (2, 0), (0, 0), (0, 0), (0, 0)))
    from_right = shifted(window_acc[:, 0].astype(jnp.bfloat16), "seq", -1).astype(jnp.float32)
    from_left = shifted(window_acc[:, block_rows + 1].astype(jnp.bfloat16), "seq", 1).astype(jnp.float32)

    kv_grad = window_acc[:, 1 : block_rows + 1]
    kv_grad = kv_grad.at[:, block_rows - 1].add(from_right).at[:, 0].add(from_left)
    oh_back = onehot(asked_flat, table_rows).T
    collected = jnp.stack(
        [
            jnp.einsum("qs,ste->qte", oh_back, returned_k, preferred_element_type=jnp.float32),
            jnp.einsum("qs,ste->qte", oh_back, returned_v, preferred_element_type=jnp.float32),
        ]
    ).reshape(2, block_rows, kv_dev, BLK, HD)
    kv_grad = kv_grad + collected.transpose(0, 1, 3, 2, 4)
    key_rest = unrotate(kv_grad[0].reshape(tok_rows, kv_dev, HD), cosines, sine_vals)
    key_rest = key_rest.reshape(block_rows, BLK, kv_dev, HD)
    value_rest = kv_grad[1]
    glob_mine = jnp.where((glob_owner == my_index)[:, None, None, None, None], glob_grad, 0.0)
    for which_glob in range(GLOB):
        glob_keys = unrotate(glob_mine[which_glob, 0], glob_cos[which_glob], glob_sin[which_glob])
        key_rest = key_rest.at[glob_local[which_glob]].add(glob_keys)
        value_rest = value_rest.at[glob_local[which_glob]].add(glob_mine[which_glob, 1])

    attended = attended.reshape(tok_rows, kv_dev * GROUP * HD)
    key_grad = key_rest.astype(jnp.bfloat16).reshape(tok_rows, kv_dev * HD)
    value_grad = value_rest.reshape(tok_rows, kv_dev * HD).astype(jnp.bfloat16)
    return (attended, query_grad, key_grad, value_grad)


def solution(mesh):
    in_specs = (
        P("seq", "head"),
        P("seq", "head"),
        P("seq", "head"),
        P(None, "seq"),
        P("seq", "head", None),
        P(),
        P("seq", "head"),
    )
    out_specs = (P("seq", "head"), P("seq", "head"), P("seq", "head"), P("seq", "head"))
    return jax.shard_map(local, mesh=mesh, in_specs=in_specs, out_specs=out_specs, check_vma=False)
```

```python
import math

import jax
import jax.numpy as jnp
from jax import lax
from jax.sharding import PartitionSpec as P

HD = 128
GROUP = 4
BLK = 64
GLOB = 2
RND = 3


NEG_FILL = -1e30
ROPE_BASE = 1000000.0


def extended(array, sides, width):
    for axis, dim in sides:
        devices, length = (lax.axis_size(axis), array.shape[dim])
        up = [(i, (i + 1) % devices) for i in range(devices - 1)]
        down = [(j, i) for i, j in up]
        last = lax.slice_in_dim(array, length - width, length, axis=dim)
        leading = lax.slice_in_dim(array, 0, width, axis=dim)
        before = lax.ppermute(last, axis, up)
        after = lax.ppermute(leading, axis, down)
        array = jnp.concatenate([before, array, after], axis=dim)
    return array


def spread(block, axis, source):
    block = jnp.where(lax.axis_index(axis) == source, block, jnp.zeros_like(block))
    return lax.psum(block, axis)


def shifted(array, axis, by):
    devices = lax.axis_size(axis)
    pairs = [(i, i + by) for i in range(devices) if 0 <= i + by < devices]
    return lax.ppermute(array, axis, pairs)


def tables(positions):
    half_dim = HD // 2
    freq_ids = jnp.arange(half_dim)
    inv_freq = jnp.power(jnp.float32(ROPE_BASE), -2.0 * freq_ids.astype(jnp.float32) / HD)
    pos_float = positions.astype(jnp.float32)
    chosen = jnp.where(
        (freq_ids % 3 == 0)[None, :],
        pos_float[0][:, None],
        jnp.where((freq_ids % 3 == 1)[None, :], pos_float[1][:, None], pos_float[2][:, None]),
    )
    angles = chosen * inv_freq[None, :]
    return (jnp.cos(angles), jnp.sin(angles))


def rotate(states, cosines, sine_vals):
    half_dim = HD // 2
    first_half = states[..., :half_dim]
    second_half = states[..., half_dim:]
    cos_b = cosines[:, None, :]
    sin_b = sine_vals[:, None, :]
    return jnp.concatenate(
        [first_half * cos_b - second_half * sin_b, second_half * cos_b + first_half * sin_b],
        axis=-1,
    )


def unrotate(states, cosines, sine_vals):
    half_dim = HD // 2
    first_half = states[..., :half_dim]
    second_half = states[..., half_dim:]
    cos_b = cosines[:, None, :]
    sin_b = sine_vals[:, None, :]
    return jnp.concatenate(
        [first_half * cos_b + second_half * sin_b, second_half * cos_b - first_half * sin_b],
        axis=-1,
    )


def attend(query_block_view, key_block_view, value_block_view, gradient_block_view, key_mask):
    score_scale = 1.0 / math.sqrt(HD)
    logit_scores = (
        jnp.einsum(
            "mtyp,mop->myto", query_block_view, key_block_view, preferred_element_type=jnp.float32
        )
        * score_scale
    )
    logit_scores = jnp.where(key_mask[:, None, None, :], logit_scores, NEG_FILL)
    row_max = jnp.max(logit_scores, axis=-1, keepdims=True)
    exponent = jnp.exp(logit_scores - row_max)
    probability = exponent / jnp.sum(exponent, axis=-1, keepdims=True)
    attention_weights = probability.astype(jnp.bfloat16)
    attended = jnp.einsum(
        "ywiu,yuz->yiwz", attention_weights, value_block_view, preferred_element_type=jnp.float32
    ).astype(jnp.bfloat16)
    weight_gradient = jnp.einsum(
        "mtyp,mop->myto", gradient_block_view, value_block_view, preferred_element_type=jnp.float32
    )
    row_delta = jnp.sum(
        gradient_block_view.astype(jnp.float32) * attended.astype(jnp.float32), axis=-1
    )
    row_delta = jnp.transpose(row_delta, (0, 2, 1))[..., None]
    score_gradient = (probability * (weight_gradient - row_delta) * score_scale).astype(
        jnp.bfloat16
    )
    value_portion = jnp.einsum(
        "pcht,phca->pta", attention_weights, gradient_block_view, preferred_element_type=jnp.float32
    )
    key_portion = jnp.einsum(
        "pcht,phca->pta", score_gradient, query_block_view, preferred_element_type=jnp.float32
    )
    query_portion = jnp.einsum(
        "ywiu,yuz->yiwz", score_gradient, key_block_view, preferred_element_type=jnp.float32
    )
    return (attended, query_portion, key_portion, value_portion)


def onehot(ids, count):
    return (ids[:, None] == jnp.arange(count, dtype=jnp.int32)[None, :]).astype(jnp.bfloat16)


def exchange(array):
    return lax.all_to_all(array, "seq", 0, 0, tiled=True)


def local(queries, key_states, value_states, positions, random_blocks, global_blocks, out_grad):
    tok_rows = queries.shape[0]
    block_rows = tok_rows // BLK
    kv_dev = key_states.shape[1] // HD
    seq_count = lax.axis_size("seq")
    my_index = lax.axis_index("seq")
    slot_count = block_rows * kv_dev * RND
    capacity = (slot_count + seq_count - 1) // seq_count + 1
    score_scale = 1.0 / math.sqrt(HD)
    table_rows = block_rows * kv_dev
    piece = 2 * BLK * kv_dev * HD // seq_count
    glob_rows = GLOB * piece // HD
    code_cols = 128

    cosines, sine_vals = tables(positions)
    q_rot = rotate(
        queries.reshape(tok_rows, kv_dev * GROUP, HD).astype(jnp.float32), cosines, sine_vals
    ).astype(jnp.bfloat16)
    k_rot = rotate(
        key_states.reshape(tok_rows, kv_dev, HD).astype(jnp.float32), cosines, sine_vals
    ).astype(jnp.bfloat16)
    paired = jnp.stack([k_rot.reshape(tok_rows, kv_dev * HD), value_states])
    own_blocks = paired.reshape(2, block_rows, BLK, kv_dev, HD)

    flat_ids = random_blocks.reshape(slot_count)
    owners = flat_ids // block_rows
    head_ids = jnp.broadcast_to(
        jnp.arange(kv_dev, dtype=jnp.int32)[None, :, None], (block_rows, kv_dev, RND)
    ).reshape(slot_count)
    req_code = flat_ids % block_rows * kv_dev + head_ids
    slot_ids = jnp.arange(slot_count, dtype=jnp.int32)
    earlier = (owners[:, None] == owners[None, :]) & (slot_ids[None, :] < slot_ids[:, None])
    slot_pos = owners * capacity + jnp.sum(earlier, axis=1)
    request = jnp.sum(
        jnp.where(
            slot_pos[None, :] == jnp.arange(seq_count * capacity, dtype=jnp.int32)[:, None],
            req_code[None, :],
            0,
        ),
        axis=1,
    ).reshape(seq_count, capacity)
    glob_owner = global_blocks // block_rows
    glob_local = global_blocks % block_rows
    glob_tokens = (glob_local[:, None] * BLK + jnp.arange(BLK, dtype=jnp.int32)[None, :]).reshape(GLOB * BLK)
    both_cos, both_sin = tables(positions[:, glob_tokens])
    glob_cos = [both_cos[g * BLK : (g + 1) * BLK] for g in range(GLOB)]
    glob_sin = [both_sin[g * BLK : (g + 1) * BLK] for g in range(GLOB)]
    glob_keys = rotate(
        key_states[glob_tokens].reshape(GLOB * BLK, kv_dev, HD).astype(jnp.float32), both_cos, both_sin
    ).astype(jnp.bfloat16)
    glob_values = value_states[glob_tokens].reshape(GLOB * BLK, kv_dev, HD)
    glob_both = jnp.stack([glob_keys, glob_values]).reshape(2, GLOB, BLK, kv_dev, HD)
    glob_both = jnp.where(
        (my_index == glob_owner)[None, :, None, None, None], glob_both, jnp.zeros_like(glob_both)
    )
    glob_scatter = [
        glob_both.transpose(1, 0, 2, 3, 4).reshape(GLOB, seq_count, piece).transpose(1, 0, 2).reshape(
            seq_count, GLOB * piece
        )
    ]
    first_out = jnp.concatenate(
        glob_scatter
        + [request.astype(jnp.bfloat16), jnp.zeros((seq_count, code_cols - capacity), jnp.bfloat16)],
        axis=1,
    )
    first_in = exchange(first_out)
    asked_part = first_in[:, GLOB * piece : GLOB * piece + capacity].astype(jnp.int32)
    my_pieces = jnp.concatenate(
        [
            lax.dynamic_index_in_dim(first_in, glob_owner[g], 0, keepdims=False)[g * piece : (g + 1) * piece]
            for g in range(GLOB)
        ]
    )
    asked_flat = asked_part.reshape(seq_count * capacity)

    k_table = own_blocks[0].transpose(0, 2, 1, 3).reshape(table_rows, BLK, HD)
    v_table = own_blocks[1].transpose(0, 2, 1, 3).reshape(table_rows, BLK, HD)
    slab_table = jnp.concatenate(
        [k_table.reshape(table_rows * BLK // glob_rows, glob_rows, HD), my_pieces.reshape(1, glob_rows, HD)]
    )
    slab_ids = (asked_part[:, :, None] * (BLK // glob_rows) + jnp.arange(BLK // glob_rows)[None, None, :])
    slab_ids = jnp.concatenate(
        [
            slab_ids.reshape(seq_count, capacity * BLK // glob_rows),
            jnp.full((seq_count, 1), table_rows * BLK // glob_rows, jnp.int32),
        ],
        axis=1,
    )
    answers_k = slab_table[slab_ids].reshape(seq_count, capacity * BLK + glob_rows, HD)
    answers_v = v_table[asked_flat].reshape(seq_count, capacity * BLK, HD)
    padded = extended(paired, (("seq", 1),), BLK)
    answers_k, padded = lax.optimization_barrier((answers_k, padded))
    fetched_k = exchange(answers_k)
    answers_v, fetched_k = lax.optimization_barrier((answers_v, fetched_k))
    fetched_v = exchange(answers_v).reshape(seq_count * capacity, BLK, HD)
    glob_in = fetched_k[:, capacity * BLK :].reshape(seq_count, GLOB, piece)
    fetched_k = fetched_k[:, : capacity * BLK].reshape(seq_count * capacity, BLK, HD)
    glob_kv = glob_in.transpose(1, 0, 2).reshape(GLOB, 2, BLK, kv_dev, HD).transpose(1, 0, 2, 3, 4)

    window_blocks = padded.reshape(2, block_rows + 2, BLK, kv_dev, HD)
    window_set = jnp.stack([window_blocks[:, offset : offset + block_rows] for offset in range(3)], axis=2)
    glob_set = jnp.broadcast_to(glob_kv[:, None], (2, block_rows, GLOB, BLK, kv_dev, HD))
    near_set = jnp.concatenate([window_set, glob_set], axis=2).reshape(
        2, block_rows, (3 + GLOB) * BLK, kv_dev, HD
    )
    window_ids = (
        my_index * block_rows + jnp.arange(block_rows)[:, None] + jnp.arange(-1, 2)[None, :]
    )
    window_ok = (window_ids >= 0) & (window_ids < seq_count * block_rows)
    near_ok = jnp.concatenate([window_ok, jnp.ones((block_rows, GLOB), dtype=bool)], axis=1)
    near_mask = jnp.repeat(near_ok, BLK, axis=1)

    query_nat = q_rot.reshape(block_rows, BLK, kv_dev, GROUP, HD)
    grad_nat = out_grad.reshape(block_rows, BLK, kv_dev, GROUP, HD)
    near_k = near_set[0]
    near_v = near_set[1]
    far_k = fetched_k[slot_pos].reshape(block_rows, kv_dev, RND * BLK, HD)
    far_v = fetched_v[slot_pos].reshape(block_rows, kv_dev, RND * BLK, HD)
    near_scores = (
        jnp.einsum("rthgd,rkhd->rhgtk", query_nat, near_k, preferred_element_type=jnp.float32)
        * score_scale
    )
    near_scores = jnp.where(near_mask[:, None, None, None, :], near_scores, NEG_FILL)
    far_scores = (
        jnp.einsum("rthgd,rhkd->rhgtk", query_nat, far_k, preferred_element_type=jnp.float32)
        * score_scale
    )
    row_max = jnp.maximum(
        jnp.max(near_scores, axis=-1, keepdims=True), jnp.max(far_scores, axis=-1, keepdims=True)
    )
    near_exp = jnp.exp(near_scores - row_max)
    far_exp = jnp.exp(far_scores - row_max)
    total = jnp.sum(near_exp, axis=-1, keepdims=True) + jnp.sum(far_exp, axis=-1, keepdims=True)
    near_prob = near_exp / total
    far_prob = far_exp / total
    near_w = near_prob.astype(jnp.bfloat16)
    far_w = far_prob.astype(jnp.bfloat16)

    far_vgrad = jnp.einsum("rhgtk,rthgd->rhkd", far_w, grad_nat, preferred_element_type=jnp.float32)
    out_v = jnp.einsum(
        "ps,pte->ste",
        onehot(slot_pos, seq_count * capacity),
        far_vgrad.astype(jnp.bfloat16).reshape(slot_count, BLK, HD),
        preferred_element_type=jnp.float32,
    ).astype(jnp.bfloat16)
    returned_v = exchange(out_v.reshape(seq_count, capacity * BLK, HD)).reshape(
        seq_count * capacity, BLK, HD
    )

    near_wgrad = jnp.einsum("rthgd,rkhd->rhgtk", grad_nat, near_v, preferred_element_type=jnp.float32)
    far_wgrad = jnp.einsum("rthgd,rhkd->rhgtk", grad_nat, far_v, preferred_element_type=jnp.float32)
    attended = (
        jnp.einsum("rhgtk,rkhd->rthgd", near_w, near_v, preferred_element_type=jnp.float32)
        + jnp.einsum("rhgtk,rhkd->rthgd", far_w, far_v, preferred_element_type=jnp.float32)
    ).astype(jnp.bfloat16)
    row_delta = jnp.sum(grad_nat.astype(jnp.float32) * attended.astype(jnp.float32), axis=-1)
    row_delta = row_delta.transpose(0, 2, 3, 1)[..., None]
    near_sgrad = (near_prob * (near_wgrad - row_delta) * score_scale).astype(jnp.bfloat16)
    far_sgrad = (far_prob * (far_wgrad - row_delta) * score_scale).astype(jnp.bfloat16)

    far_kgrad = jnp.einsum("rhgtk,rthgd->rhkd", far_sgrad, query_nat, preferred_element_type=jnp.float32)
    out_k = jnp.einsum(
        "ps,pte->ste",
        onehot(slot_pos, seq_count * capacity),
        far_kgrad.astype(jnp.bfloat16).reshape(slot_count, BLK, HD),
        preferred_element_type=jnp.float32,
    ).astype(jnp.bfloat16).reshape(seq_count, capacity * BLK, HD)
    near_kgrad = jnp.einsum("rhgtk,rthgd->rkhd", near_sgrad, query_nat, preferred_element_type=jnp.float32)
    near_vgrad = jnp.einsum("rhgtk,rthgd->rkhd", near_w, grad_nat, preferred_element_type=jnp.float32)
    near_grad = jnp.stack([near_kgrad, near_vgrad]).reshape(2, block_rows, 3 + GLOB, BLK, kv_dev, HD)
    glob_local_grad = jnp.sum(near_grad[:, :, 3:], axis=1)
    glob_split = glob_local_grad.transpose(1, 0, 2, 3, 4).reshape(GLOB, seq_count, piece)
    glob_split = glob_split.transpose(1, 0, 2).reshape(seq_count, glob_rows, HD)
    glob_high = glob_split.astype(jnp.bfloat16)
    glob_low = (glob_split - glob_high.astype(jnp.float32)).astype(jnp.bfloat16)
    query_portion = jnp.einsum(
        "rhgtk,rkhd->rthgd", near_sgrad, near_k, preferred_element_type=jnp.float32
    ) + jnp.einsum("rhgtk,rhkd->rthgd", far_sgrad, far_k, preferred_element_type=jnp.float32)
    query_grad = (
        unrotate(query_portion.reshape(tok_rows, kv_dev * GROUP, HD), cosines, sine_vals)
        .astype(jnp.bfloat16)
        .reshape(tok_rows, kv_dev * GROUP * HD)
    )
    payload_k = jnp.concatenate([out_k, glob_high, glob_low], axis=1)
    payload_k, query_grad = lax.optimization_barrier((payload_k, query_grad))
    returned_k = exchange(payload_k)
    glob_back = returned_k[:, capacity * BLK :].astype(jnp.float32)
    piece_sum = jnp.sum(glob_back[:, :glob_rows] + glob_back[:, glob_rows:], axis=0).reshape(GLOB, piece)
    returned_k = returned_k[:, : capacity * BLK].reshape(seq_count * capacity, BLK, HD)
    to_owner = jnp.where(
        jnp.arange(seq_count)[:, None, None] == glob_owner[None, :, None], piece_sum[None], 0.0
    )
    to_owner = to_owner.reshape(seq_count, glob_rows, HD)
    glob_grad = exchange(to_owner).reshape(seq_count, GLOB, piece)
    glob_grad = glob_grad.transpose(1, 0, 2).reshape(GLOB, 2, BLK, kv_dev, HD)

    window_acc = jnp.pad(near_grad[:, :, 0], ((0, 0), (0, 2), (0, 0), (0, 0), (0, 0)))
    window_acc = window_acc + jnp.pad(near_grad[:, :, 1], ((0, 0), (1, 1), (0, 0), (0, 0), (0, 0)))
    window_acc = window_acc + jnp.pad(near_grad[:, :, 2], ((0, 0), (2, 0), (0, 0), (0, 0), (0, 0)))
    from_right = shifted(window_acc[:, 0].astype(jnp.bfloat16), "seq", -1).astype(jnp.float32)
    from_left = shifted(window_acc[:, block_rows + 1].astype(jnp.bfloat16), "seq", 1).astype(jnp.float32)

    kv_grad = window_acc[:, 1 : block_rows + 1]
    kv_grad = kv_grad.at[:, block_rows - 1].add(from_right).at[:, 0].add(from_left)
    oh_back = onehot(asked_flat, table_rows).T
    collected = jnp.stack(
        [
            jnp.einsum("qs,ste->qte", oh_back, returned_k, preferred_element_type=jnp.float32),
            jnp.einsum("qs,ste->qte", oh_back, returned_v, preferred_element_type=jnp.float32),
        ]
    ).reshape(2, block_rows, kv_dev, BLK, HD)
    kv_grad = kv_grad + collected.transpose(0, 1, 3, 2, 4)
    key_rest = unrotate(kv_grad[0].reshape(tok_rows, kv_dev, HD), cosines, sine_vals)
    key_rest = key_rest.reshape(block_rows, BLK, kv_dev, HD)
    value_rest = kv_grad[1]
    glob_mine = jnp.where((glob_owner == my_index)[:, None, None, None, None], glob_grad, 0.0)
    for which_glob in range(GLOB):
        glob_keys = unrotate(glob_mine[which_glob, 0], glob_cos[which_glob], glob_sin[which_glob])
        key_rest = key_rest.at[glob_local[which_glob]].add(glob_keys)
        value_rest = value_rest.at[glob_local[which_glob]].add(glob_mine[which_glob, 1])

    attended = attended.reshape(tok_rows, kv_dev * GROUP * HD)
    key_grad = key_rest.astype(jnp.bfloat16).reshape(tok_rows, kv_dev * HD)
    value_grad = value_rest.reshape(tok_rows, kv_dev * HD).astype(jnp.bfloat16)
    return (attended, query_grad, key_grad, value_grad)


def solution(mesh):
    in_specs = (
        P("seq", "head"),
        P("seq", "head"),
        P("seq", "head"),
        P(None, "seq"),
        P("seq", "head", None),
        P(),
        P("seq", "head"),
    )
    out_specs = (P("seq", "head"), P("seq", "head"), P("seq", "head"), P("seq", "head"))
    return jax.shard_map(local, mesh=mesh, in_specs=in_specs, out_specs=out_specs, check_vma=False)
```
